128 devices in a mesh: dom: 32 (over y, x, core), band: 4 (over z).
Axes of the slice: x: 4, y: 4, z: 4, core: 2. Of those that a mesh axis runs over, the one named last changes fastest.
Arguments:
- states: bfloat16 [256, 393216], P('band', 'dom'), may hold values from -640 to 640
- cell_kinetic: bfloat16 [512, 512], replicated, may hold values from -0.3 to 0.3, as said below
- cell_scale: float32 [1024], P('dom'), may hold values from 0.5 to 2
- cell_potential: float32 [1024, 512], P('dom'), may hold values from -0.3 to 0.3
- connectivity: int32 [1024, 512], P('dom'), may hold values from 0 to 12287, as said below
- shared_nodes: int32 [32, 2, 1024], P('dom'), may hold values from 0 to 12287, as said below
- cell_counts: int32 [32], P('dom'), may hold values from 4 to 32, as said below
Outputs:
- rotated: bfloat16 [256, 393216], P('band', 'dom')
The draws below stay inside these ranges and needn't reach their ends.
Inputs may be any that keep to these rules, and one draw needn't show every extreme that they name: cell_kinetic is symmetric. `connectivity`: row c of a domain (local cell number c) names each of the 512 nodes c * 3 * 128 to c * 3 * 128 + 511, counted round modulo 12288, exactly once. `shared_nodes`: the two rows of a domain name 2048 distinct nodes; position p of domain d's row 1 and of domain d+1's row 0 are the same physical node. `cell_counts`: in every draw some domain has all 32 cells live.
All inputs are finite; a program needn't handle non-finite values.
Results may differ from the reference program's by a relative error of at most 0.008.
Values may be sent and summed in bfloat16 or wider, within the bound.
No kernel may reach another device: no remote copies, remote signals or barrier semaphores. Data moves between devices by JAX's collectives and lax.ppermute only.
A program may use at most 128 MiB of HBM per device.

```python
import math
import jax
import jax.numpy as jnp
from jax import lax

NP = 512
S = 256
CELLS_DEV = 32
CHEB = 4
NS_ITERS = 5
NODES = 12288
SHARED = 1024
CELLS = 1024
NODES_ALL = 393216
N_DOM = 32


def draw_states(key, part):
    base_key, state_key = jax.random.split(key, 2)
    pair_key = jax.random.fold_in(key, 31)
    node_scale = 1.0 + 0.75 * jnp.arange(NODES_ALL, dtype=jnp.float32) / NODES_ALL
    state_scale = jnp.exp(jax.random.uniform(state_key, (S,), jnp.float32, 0.0, math.log(10.0)))
    offset = jax.random.randint(pair_key, (), 0, N_DOM, dtype=jnp.int32)
    partner = (jnp.arange(S, dtype=jnp.int32) + offset) % N_DOM
    node_domain = jnp.arange(NODES_ALL, dtype=jnp.int32) // NODES
    spike = jnp.where(node_domain[None, :] == partner[:, None], 6.0, 1.0).astype(jnp.float32)
    values = jnp.clip(jax.random.normal(base_key, (S, NODES_ALL), jnp.float32), -6.0, 6.0)
    return (values * spike * state_scale[:, None] * node_scale[None]).astype(jnp.bfloat16)


def draw_cell_kinetic(key, part):
    raw = jnp.clip(jax.random.normal(key, (NP, NP), jnp.float32), -4.0, 4.0)
    return (0.15 * jnp.eye(NP, dtype=jnp.float32) + (raw + raw.T) * (0.1 / math.sqrt(NP))).astype(jnp.bfloat16)


def draw_connectivity(key, part):
    order_key = jax.random.fold_in(key, 11)
    local_cell = jnp.arange(CELLS, dtype=jnp.int32) % CELLS_DEV
    window = jax.random.permutation(order_key, jnp.broadcast_to(jnp.arange(NP, dtype=jnp.int32), (CELLS, NP)), axis=1, independent=True)
    return (local_cell[:, None] * (NP * 3 // 4) + window) % NODES


def draw_shared_nodes(key, part):
    shuffled = jax.random.permutation(key, jnp.broadcast_to(jnp.arange(NODES, dtype=jnp.int32), (N_DOM, NODES)), axis=1, independent=True)
    return jnp.stack([shuffled[:, :SHARED], shuffled[:, SHARED:2 * SHARED]], axis=1)


def draw_cell_counts(key, part):
    first_key = jax.random.fold_in(key, 21)
    second_key = jax.random.fold_in(key, 22)
    full_key = jax.random.fold_in(key, 23)
    lowest = max(1, CELLS_DEV // 8)
    first = jax.random.randint(first_key, (N_DOM,), lowest, CELLS_DEV + 1, dtype=jnp.int32)
    second = jax.random.randint(second_key, (N_DOM,), lowest, CELLS_DEV + 1, dtype=jnp.int32)
    counts = jnp.minimum(first, second)
    fullest = jax.random.randint(full_key, (), 0, N_DOM, dtype=jnp.int32)
    return counts.at[fullest].set(CELLS_DEV)


def level_of(key, shape, shards, low, largest):
    loudness, own = 1.0, jax.random.fold_in(key, 6)
    for dim, blocks in shards:
        draws = jnp.exp(jax.random.uniform(jax.random.fold_in(own, dim), (blocks,), jnp.float32, low / len(shards), largest / len(shards)))
        loudness = loudness * jnp.repeat(draws, shape[dim] // blocks).reshape([-1 if axis == dim else 1 for axis in range(len(shape))])
    return loudness


def setup_inputs(seed: int = 0) -> dict:
    splits = jax.random.split(jax.random.key(seed), 8)
    states = draw_states(jax.random.fold_in(splits[7], 71), 0)
    cell_kinetic = draw_cell_kinetic(jax.random.fold_in(splits[7], 71), 0)
    cell_scale = jnp.clip(jnp.exp(math.log(2.0) - 1.3862944 * jax.random.uniform(splits[2], (CELLS,), jnp.float32) ** level_of(splits[2], (CELLS,), ((0, 32),), -0.2, 0.2)), 0.5, 2.0)
    cell_potential = jnp.clip(jax.random.uniform(splits[3], (CELLS, NP), jnp.float32, -0.3, 0.3) * level_of(splits[3], (CELLS, NP), ((0, 32),), -0.4, 0.0), -0.3, 0.3)
    connectivity = draw_connectivity(jax.random.fold_in(splits[7], 71), 0)
    shared_nodes = draw_shared_nodes(jax.random.fold_in(splits[7], 71), 0)
    cell_counts = draw_cell_counts(jax.random.fold_in(splits[7], 71), 0)
    return {"states": states, "cell_kinetic": cell_kinetic, "cell_scale": cell_scale, "cell_potential": cell_potential, "connectivity": connectivity, "shared_nodes": shared_nodes, "cell_counts": cell_counts}


def pick_columns(field, positions):
    return field[:, positions]

def add_faces(field, left_row, right_row, left_add, right_add):
    return field.at[:, left_row].add(left_add).at[:, right_row].add(right_add)

def count_uses(left_row, right_row, left_flag, right_flag):
    return jnp.ones((NODES,), jnp.float32).at[left_row].add(left_flag).at[right_row].add(right_flag)

def reference(states, cell_kinetic, cell_scale, cell_potential, connectivity, shared_nodes, cell_counts):
    kinetic = cell_kinetic.astype(jnp.float32)
    scales = cell_scale.reshape(N_DOM, CELLS_DEV)
    potential = cell_potential.reshape(N_DOM, CELLS_DEV, NP)
    connect = connectivity.reshape(N_DOM, CELLS_DEV, NP)
    left_face = shared_nodes[:, 0]
    right_face = shared_nodes[:, 1]

    def local_domain(packed):
        vector, scale_row, potential_rows, conn_rows, live_count = packed
        gathered = vector[:, conn_rows].astype(jnp.float32)
        product = jnp.einsum('scj,ij->sci', gathered, kinetic)
        alive_mask = (jnp.arange(CELLS_DEV) < live_count).astype(jnp.float32)
        cell_terms = (product * scale_row[None, :, None] + potential_rows[None] * gathered) * alive_mask[None, :, None]
        return jnp.zeros((S, NODES), jnp.float32).at[:, conn_rows].add(cell_terms)

    def apply_field(fields):
        local_sum = lax.map(local_domain, (fields, scales, potential, connect, cell_counts))
        right_values = jax.vmap(pick_columns)(local_sum, right_face)
        left_values = jax.vmap(pick_columns)(local_sum, left_face)
        zero_face = jnp.zeros_like(right_values[:1])
        from_left = jnp.concatenate([zero_face, right_values[:-1]], axis=0)
        from_right = jnp.concatenate([left_values[1:], zero_face], axis=0)
        return jax.vmap(add_faces)(local_sum, left_face, right_face, from_left, from_right)
    fields = states.reshape(S, N_DOM, NODES).transpose(1, 0, 2)
    previous = fields
    current = apply_field(fields).astype(jnp.bfloat16)
    for repeat in range(CHEB - 1):
        following = (2.0 * apply_field(current) - previous.astype(jnp.float32)).astype(jnp.bfloat16)
        previous = current
        current = following
    has_left = (jnp.arange(N_DOM) > 0).astype(jnp.float32)
    has_right = (jnp.arange(N_DOM) < N_DOM - 1).astype(jnp.float32)
    multiplicity = jax.vmap(count_uses)(left_face, right_face, has_left, has_right)
    node_weight = (1.0 / multiplicity).astype(jnp.bfloat16)

    def add_domain(carry, packed):
        field, weight_row = packed
        weighted = field * weight_row[None]
        return (carry + jnp.dot(weighted, field.T, preferred_element_type=jnp.float32), None)
    gram_matrix, unused = lax.scan(add_domain, jnp.zeros((S, S), jnp.float32), (current, node_weight))
    identity = jnp.eye(S, dtype=jnp.float32)
    frobenius = jnp.sqrt(jnp.sum(gram_matrix * gram_matrix))
    scaled = gram_matrix / frobenius
    inverse_root = identity
    for repeat in range(NS_ITERS):
        factor = 1.5 * identity - 0.5 * jnp.dot(inverse_root, scaled, precision=lax.Precision.HIGHEST)
        scaled = jnp.dot(scaled, factor, precision=lax.Precision.HIGHEST)
        inverse_root = jnp.dot(factor, inverse_root, precision=lax.Precision.HIGHEST)
    mixing = inverse_root.astype(jnp.bfloat16)

    def rotate_domain(field):
        return jnp.dot(mixing.T, field, preferred_element_type=jnp.float32).astype(jnp.bfloat16)
    rotated = lax.map(rotate_domain, current)
    return rotated.transpose(1, 0, 2).reshape(S, NODES_ALL)
```

```python
import jax
import jax.numpy as jnp
from jax import lax
from jax.sharding import PartitionSpec as P

CHEB = 4
NS_ITERS = 5


def window_operators(connectivity, cell_kinetic, cell_potential, node_total):
    cell_total = connectivity.shape[0]
    width = connectivity.shape[1]
    quarter = width // 4
    starts = jnp.arange(cell_total, dtype=jnp.int32) * (3 * quarter)
    slots = (connectivity - starts[:, None]) % node_total
    onehot = (slots[:, :, None] == jnp.arange(width, dtype=jnp.int32)[None, None, :]).astype(
        jnp.bfloat16
    )
    kinetic_cols = jnp.einsum(
        "ij,cia->cja", cell_kinetic, onehot, preferred_element_type=jnp.float32
    ).astype(jnp.bfloat16)
    window_ops = jnp.einsum(
        "cjb,cja->cba", onehot, kinetic_cols, preferred_element_type=jnp.float32
    ).astype(jnp.bfloat16)
    window_pot = jnp.einsum(
        "ci,cia->ca", cell_potential, onehot.astype(jnp.float32), precision=lax.Precision.HIGHEST
    )
    return (window_ops, window_pot)


def local_apply(vector, window_ops, window_pot, scales):
    node_total, state_cols = vector.shape
    cell_total, width = window_pot.shape
    quarter = width // 4
    blocked = vector.reshape(cell_total, 3, quarter, state_cols)
    following = jnp.roll(blocked[:, 0], -1, axis=0)
    windows = jnp.concatenate([blocked, following[:, None]], axis=1).reshape(
        cell_total, width, state_cols
    )
    product = jnp.einsum(
        "cba,cbs->cas", window_ops, windows, preferred_element_type=jnp.float32
    )
    terms = product * scales[:, None, None] + window_pot[:, :, None] * windows.astype(jnp.float32)
    split_terms = terms.reshape(cell_total, 4, quarter, state_cols)
    first = split_terms[:, 0] + jnp.roll(split_terms[:, 3], 1, axis=0)
    folded = jnp.concatenate([first[:, None], split_terms[:, 1:3]], axis=1)
    return folded.reshape(node_total, state_cols)


def newton(gram_matrix):
    identity = jnp.eye(gram_matrix.shape[0], dtype=jnp.float32)
    frobenius = jnp.sqrt(jnp.sum(gram_matrix * gram_matrix))
    scaled = gram_matrix / frobenius
    inverse_root = identity
    for repeat in range(NS_ITERS):
        factor = 1.5 * identity - 0.5 * jnp.dot(
            inverse_root, scaled, precision=lax.Precision.HIGHEST
        )
        scaled = jnp.dot(scaled, factor, precision=lax.Precision.HIGHEST)
        inverse_root = jnp.dot(factor, inverse_root, precision=lax.Precision.HIGHEST)
    return inverse_root.astype(jnp.bfloat16)


def butterfly_sum(value):
    band_size = lax.axis_size("band")
    count = lax.axis_size("dom") * band_size
    index = lax.axis_index("dom") * band_size + lax.axis_index("band")
    bits = [b for b in range(count.bit_length() - 1)]
    order = bits[2:3] + bits[0:2] + bits[3:]
    buffer = value.reshape(-1)
    kept = []
    for bit in order:
        mask = 1 << bit
        pairs = [(i, i ^ mask) for i in range(count)]
        half = buffer.shape[0] // 2
        low, high = buffer[:half], buffer[half:]
        upper = (index & mask) != 0
        received = lax.ppermute(jnp.where(upper, low, high), ("dom", "band"), pairs)
        buffer = jnp.where(upper, high, low) + received
        kept.append((mask, upper))
    for mask, upper in reversed(kept):
        pairs = [(i, i ^ mask) for i in range(count)]
        received = lax.ppermute(buffer, ("dom", "band"), pairs)
        buffer = jnp.where(
            upper,
            jnp.concatenate([received, buffer]),
            jnp.concatenate([buffer, received]),
        )
    return buffer.reshape(value.shape)


def body(states, cell_kinetic, cell_scale, cell_potential, connectivity, shared_nodes, cell_counts):
    left_face = shared_nodes[0, 0]
    right_face = shared_nodes[0, 1]
    face_width = left_face.shape[0]
    faces = jnp.concatenate([left_face, right_face])
    live_count = cell_counts[0]
    domain = lax.axis_index("dom")
    domains = lax.axis_size("dom")
    node_total = states.shape[1]
    has_left = (domain > 0).astype(jnp.float32)
    has_right = (domain < domains - 1).astype(jnp.float32)
    multiplicity = (
        jnp.ones((node_total,), jnp.float32)
        .at[left_face]
        .add(has_left)
        .at[right_face]
        .add(has_right)
    )
    node_weight = (1.0 / multiplicity).astype(jnp.bfloat16)
    window_ops, window_pot = window_operators(
        connectivity, cell_kinetic, cell_potential, node_total
    )
    alive = (jnp.arange(window_pot.shape[0]) < live_count).astype(jnp.float32)
    scales = cell_scale * alive
    window_pot = window_pot * alive[:, None]
    up = [(i, i + 1) for i in range(domains - 1)]
    down = [(j, i) for i, j in up]

    def apply_field(vector):
        local_sum = local_apply(vector, window_ops, window_pot, scales)
        face_values = jnp.take(local_sum, faces, axis=0)
        from_left = lax.ppermute(face_values[face_width:], "dom", up)
        from_right = lax.ppermute(face_values[:face_width], "dom", down)
        received = jnp.concatenate([from_left, from_right], axis=0)
        return local_sum.at[faces].add(received, unique_indices=True)

    previous = states.T
    current = apply_field(previous).astype(jnp.bfloat16)
    for repeat in range(CHEB - 1):
        following = (2.0 * apply_field(current) - previous.astype(jnp.float32)).astype(jnp.bfloat16)
        previous = current
        current = following
    row_shard = lax.all_to_all(current, "band", split_axis=0, concat_axis=1, tiled=True)
    piece_nodes = row_shard.shape[0]
    weight_rows = lax.dynamic_slice_in_dim(
        node_weight, lax.axis_index("band") * piece_nodes, piece_nodes, 0
    )
    weighted = row_shard * weight_rows[:, None]
    partial_gram = lax.dot_general(
        weighted, row_shard, (((0,), (0,)), ((), ())), preferred_element_type=jnp.float32
    )
    gram_matrix = butterfly_sum(partial_gram)
    mixing = newton(gram_matrix)
    rotated = lax.dot_general(
        row_shard, mixing, (((1,), (0,)), ((), ())), preferred_element_type=jnp.float32
    ).astype(jnp.bfloat16)
    back = lax.all_to_all(rotated, "band", split_axis=1, concat_axis=0, tiled=True)
    return back.T


def solution(mesh):
    in_specs = (
        P("band", "dom"),
        P(),
        P("dom"),
        P("dom", None),
        P("dom", None),
        P("dom", None, None),
        P("dom"),
    )
    out_specs = P("band", "dom")
    return jax.shard_map(body, mesh=mesh, in_specs=in_specs, out_specs=out_specs, check_vma=False)
```

```python
import functools

import jax
import jax.numpy as jnp
from jax import lax
from jax.experimental import pallas as pl
from jax.experimental.pallas import tpu as pltpu
from jax.sharding import PartitionSpec as P

CHEB = 4
NS_ITERS = 5


VMEM_LIMIT = 60 * 1024 * 1024


def field_kernel(combine, older, apply, alpha, *refs):
    refs = list(refs)
    faces = refs.pop(0)
    if apply:
        scales = refs.pop(0)
    if combine:
        local_in = refs.pop(0)
        received = refs.pop(0)
        if older:
            older_ref = refs.pop(0)
    else:
        vector_in = refs.pop(0)
    if apply:
        ops_ref = refs.pop(0)
        pot_ref = refs.pop(0)
    if combine:
        vector_out = refs.pop(0)
    if apply:
        local_out = refs.pop(0)
        faces_out = refs.pop(0)
    if combine:
        work = refs.pop(0)
    vector = vector_out if combine else vector_in
    face_total = faces.shape[0]
    node_total = vector.shape[0]
    cell = pl.program_id(0) if apply else None

    def prologue():
        work[...] = local_in[...] if alpha == 1.0 else alpha * local_in[...]

        def fix(p, carry):
            n = faces[p]
            row = received[pl.ds(p, 1), :]
            work[pl.ds(n, 1), :] += row if alpha == 1.0 else alpha * row
            return carry

        lax.fori_loop(0, face_total, fix, 0, unroll=8)
        value = work[...]
        if older:
            value = value - older_ref[...].astype(jnp.float32)
        vector_out[...] = value.astype(vector_out.dtype)

    if combine:
        if apply:
            pl.when(cell == 0)(prologue)
        else:
            prologue()

    if apply:
        width = ops_ref.shape[1]
        quarter = width // 4
        body_rows = width - quarter

        @pl.when(cell == 0)
        def _():
            local_out[...] = jnp.zeros_like(local_out)

        start = pl.multiple_of(cell * body_rows, quarter)
        tail = pl.multiple_of(lax.rem((cell + 1) * body_rows, node_total), quarter)
        main_rows = vector[pl.ds(start, body_rows), :]
        tail_rows = vector[pl.ds(tail, quarter), :]
        ops = ops_ref[0]
        product = jnp.dot(ops[:, :body_rows], main_rows, preferred_element_type=jnp.float32)
        product = product + jnp.dot(ops[:, body_rows:], tail_rows, preferred_element_type=jnp.float32)
        scale = scales[cell]
        pot = pot_ref[0]
        top = product[:body_rows] * scale + pot[:body_rows] * main_rows.astype(jnp.float32)
        bottom = product[body_rows:] * scale + pot[body_rows:] * tail_rows.astype(jnp.float32)
        local_out[pl.ds(start, body_rows), :] += top
        local_out[pl.ds(tail, quarter), :] += bottom

        @pl.when(cell == pl.num_programs(0) - 1)
        def _():
            def pick(p, carry):
                n = faces[p]
                faces_out[pl.ds(p, 1), :] = local_out[pl.ds(n, 1), :]
                return carry

            lax.fori_loop(0, face_total, pick, 0, unroll=8)


def field_step(faces, scales, window_ops, window_pot, vector=None, local_in=None,
               received=None, older=None, alpha=1.0, apply=True):
    combine = local_in is not None
    has_older = older is not None
    node_total, cols = (local_in if combine else vector).shape
    face_total = faces.shape[0]
    cells, width, _ = window_ops.shape
    smem = pl.BlockSpec(memory_space=pltpu.SMEM)
    whole = pl.BlockSpec(memory_space=pltpu.VMEM)
    args, specs = [faces], [smem]
    if apply:
        args.append(scales); specs.append(smem)
    if combine:
        args += [local_in, received]; specs += [whole, whole]
        if has_older:
            args.append(older); specs.append(whole)
    else:
        args.append(vector); specs.append(whole)
    if apply:
        args += [window_ops, window_pot]
        specs += [pl.BlockSpec((1, width, width), lambda c: (c, 0, 0)),
                  pl.BlockSpec((1, width, cols), lambda c: (c, 0, 0))]
    out_shape, out_specs = [], []
    if combine:
        out_shape.append(jax.ShapeDtypeStruct((node_total, cols), jnp.bfloat16)); out_specs.append(whole)
    if apply:
        out_shape += [jax.ShapeDtypeStruct((node_total, cols), jnp.float32),
                      jax.ShapeDtypeStruct((face_total, cols), jnp.float32)]
        out_specs += [whole, whole]
    scratch = [pltpu.VMEM((node_total, cols), jnp.float32)] if combine else []
    flops = 2 * cells * width * width * cols if apply else 0
    result = pl.pallas_call(
        functools.partial(field_kernel, combine, has_older, apply, alpha),
        grid=(cells if apply else 1,),
        in_specs=specs,
        out_specs=out_specs,
        out_shape=out_shape,
        scratch_shapes=scratch,
        compiler_params=pltpu.CompilerParams(
            dimension_semantics=("arbitrary",), vmem_limit_bytes=VMEM_LIMIT),
        cost_estimate=pl.CostEstimate(
            flops=flops, transcendentals=0,
            bytes_accessed=(cells * width * width * 2 if apply else 0) + node_total * cols * 12),
    )(*args)
    return result


def window_operators(connectivity, cell_kinetic, cell_potential, node_total):
    cell_total = connectivity.shape[0]
    width = connectivity.shape[1]
    quarter = width // 4
    starts = jnp.arange(cell_total, dtype=jnp.int32) * (3 * quarter)
    slots = (connectivity - starts[:, None]) % node_total
    onehot = (slots[:, :, None] == jnp.arange(width, dtype=jnp.int32)[None, None, :]).astype(
        jnp.bfloat16
    )
    kinetic_cols = jnp.einsum(
        "ij,cia->cja", cell_kinetic, onehot, preferred_element_type=jnp.float32
    ).astype(jnp.bfloat16)
    window_ops = jnp.einsum(
        "cjb,cja->cba", onehot, kinetic_cols, preferred_element_type=jnp.float32
    ).astype(jnp.bfloat16)
    window_pot = jnp.einsum(
        "ci,cia->ca", cell_potential, onehot.astype(jnp.float32), precision=lax.Precision.HIGHEST
    )
    return (window_ops, window_pot)


def newton(gram_matrix):
    identity = jnp.eye(gram_matrix.shape[0], dtype=jnp.float32)
    frobenius = jnp.sqrt(jnp.sum(gram_matrix * gram_matrix))
    scaled = gram_matrix / frobenius
    inverse_root = identity
    for repeat in range(NS_ITERS):
        factor = 1.5 * identity - 0.5 * jnp.dot(
            inverse_root, scaled, precision=lax.Precision.HIGHEST
        )
        scaled = jnp.dot(scaled, factor, precision=lax.Precision.HIGHEST)
        inverse_root = jnp.dot(factor, inverse_root, precision=lax.Precision.HIGHEST)
    return inverse_root.astype(jnp.bfloat16)


def butterfly_sum(value):
    band_size = lax.axis_size("band")
    count = lax.axis_size("dom") * band_size
    index = lax.axis_index("dom") * band_size + lax.axis_index("band")
    bits = [b for b in range(count.bit_length() - 1)]
    order = bits[2:3] + bits[0:2] + bits[3:]
    buffer = value.reshape(-1)
    kept = []
    for bit in order:
        mask = 1 << bit
        pairs = [(i, i ^ mask) for i in range(count)]
        half = buffer.shape[0] // 2
        low, high = buffer[:half], buffer[half:]
        upper = (index & mask) != 0
        received = lax.ppermute(jnp.where(upper, low, high), ("dom", "band"), pairs)
        buffer = jnp.where(upper, high, low) + received
        kept.append((mask, upper))
    for mask, upper in reversed(kept):
        pairs = [(i, i ^ mask) for i in range(count)]
        received = lax.ppermute(buffer, ("dom", "band"), pairs)
        buffer = jnp.where(
            upper,
            jnp.concatenate([received, buffer]),
            jnp.concatenate([buffer, received]),
        )
    return buffer.reshape(value.shape)


def body(states, cell_kinetic, cell_scale, cell_potential, connectivity, shared_nodes, cell_counts):
    left_face = shared_nodes[0, 0]
    right_face = shared_nodes[0, 1]
    face_width = left_face.shape[0]
    faces = jnp.concatenate([left_face, right_face])
    live_count = cell_counts[0]
    domain = lax.axis_index("dom")
    domains = lax.axis_size("dom")
    node_total = states.shape[1]
    state_cols = states.shape[0]
    has_left = (domain > 0).astype(jnp.float32)
    has_right = (domain < domains - 1).astype(jnp.float32)
    multiplicity = (
        jnp.ones((node_total,), jnp.float32)
        .at[left_face]
        .add(has_left)
        .at[right_face]
        .add(has_right)
    )
    node_weight = (1.0 / multiplicity).astype(jnp.bfloat16)
    window_ops, window_pot = window_operators(
        connectivity, cell_kinetic, cell_potential, node_total
    )
    cells, width = window_pot.shape
    alive = (jnp.arange(cells) < live_count).astype(jnp.float32)
    scales = cell_scale * alive
    window_pot = jnp.broadcast_to(
        (window_pot * alive[:, None])[:, :, None], (cells, width, state_cols)
    )
    up = [(i, i + 1) for i in range(domains - 1)]
    down = [(j, i) for i, j in up]

    def exchange(face_values):
        from_left = lax.ppermute(face_values[face_width:], "dom", up)
        from_right = lax.ppermute(face_values[:face_width], "dom", down)
        return jnp.concatenate([from_left, from_right], axis=0)

    step = functools.partial(field_step, faces, scales, window_ops, window_pot)
    first = states.T
    local_sum, face_values = step(vector=first)
    second, local_sum, face_values = step(local_in=local_sum, received=exchange(face_values))
    history = [first, second]
    for repeat in range(CHEB - 2):
        following, local_sum, face_values = step(
            local_in=local_sum, received=exchange(face_values), older=history[-2], alpha=2.0
        )
        history.append(following)
    (current,) = step(
        local_in=local_sum, received=exchange(face_values), older=history[-2], alpha=2.0,
        apply=False,
    )
    row_shard = lax.all_to_all(current, "band", split_axis=0, concat_axis=1, tiled=True)
    piece_nodes = row_shard.shape[0]
    weight_rows = lax.dynamic_slice_in_dim(
        node_weight, lax.axis_index("band") * piece_nodes, piece_nodes, 0
    )
    weighted = row_shard * weight_rows[:, None]
    partial_gram = lax.dot_general(
        weighted, row_shard, (((0,), (0,)), ((), ())), preferred_element_type=jnp.float32
    )
    gram_matrix = butterfly_sum(partial_gram)
    mixing = newton(gram_matrix)
    rotated = lax.dot_general(
        row_shard, mixing, (((1,), (0,)), ((), ())), preferred_element_type=jnp.float32
    ).astype(jnp.bfloat16)
    back = lax.all_to_all(rotated, "band", split_axis=1, concat_axis=0, tiled=True)
    return back.T


def solution(mesh):
    in_specs = (
        P("band", "dom"),
        P(),
        P("dom"),
        P("dom", None),
        P("dom", None),
        P("dom", None, None),
        P("dom"),
    )
    out_specs = P("band", "dom")
    return jax.shard_map(body, mesh=mesh, in_specs=in_specs, out_specs=out_specs, check_vma=False)
```

```python
import functools

import jax
import jax.numpy as jnp
from jax import lax
from jax.experimental import pallas as pl
from jax.experimental.pallas import tpu as pltpu
from jax.sharding import PartitionSpec as P

CHEB = 4
NS_ITERS = 5


VMEM_LIMIT = 60 * 1024 * 1024


def field_kernel(combine, older, apply, alpha, *refs):
    refs = list(refs)
    faces = refs.pop(0)
    if apply:
        scales = refs.pop(0)
    if combine:
        local_in = refs.pop(0)
        received = refs.pop(0)
        if older:
            older_ref = refs.pop(0)
    else:
        vector_in = refs.pop(0)
    if apply:
        ops_ref = refs.pop(0)
        pot_ref = refs.pop(0)
    if combine:
        vector_out = refs.pop(0)
    if apply:
        local_out = refs.pop(0)
        faces_out = refs.pop(0)
    if combine:
        work = refs.pop(0)
    vector = vector_out if combine else vector_in
    face_total = faces.shape[0]
    node_total = vector.shape[0]
    cell = pl.program_id(0) if apply else None

    def prologue():
        work[...] = local_in[...] if alpha == 1.0 else alpha * local_in[...]

        def fix(p, carry):
            n = faces[p]
            row = received[pl.ds(p, 1), :]
            work[pl.ds(n, 1), :] += row if alpha == 1.0 else alpha * row
            return carry

        lax.fori_loop(0, face_total, fix, 0, unroll=8)
        value = work[...]
        if older:
            value = value - older_ref[...].astype(jnp.float32)
        vector_out[...] = value.astype(vector_out.dtype)

    if combine:
        if apply:
            pl.when(cell == 0)(prologue)
        else:
            prologue()

    if apply:
        width = ops_ref.shape[1]
        quarter = width // 4
        body_rows = width - quarter

        @pl.when(cell == 0)
        def _():
            local_out[...] = jnp.zeros_like(local_out)

        start = pl.multiple_of(cell * body_rows, quarter)
        tail = pl.multiple_of(lax.rem((cell + 1) * body_rows, node_total), quarter)
        main_rows = vector[pl.ds(start, body_rows), :]
        tail_rows = vector[pl.ds(tail, quarter), :]
        ops = ops_ref[0]
        product = jnp.dot(ops[:, :body_rows], main_rows, preferred_element_type=jnp.float32)
        product = product + jnp.dot(ops[:, body_rows:], tail_rows, preferred_element_type=jnp.float32)
        scale = scales[cell]
        pot = pot_ref[0]
        top = product[:body_rows] * scale + pot[:body_rows] * main_rows.astype(jnp.float32)
        bottom = product[body_rows:] * scale + pot[body_rows:] * tail_rows.astype(jnp.float32)
        local_out[pl.ds(start, body_rows), :] += top
        local_out[pl.ds(tail, quarter), :] += bottom

        @pl.when(cell == pl.num_programs(0) - 1)
        def _():
            def pick(p, carry):
                n = faces[p]
                faces_out[pl.ds(p, 1), :] = local_out[pl.ds(n, 1), :]
                return carry

            lax.fori_loop(0, face_total, pick, 0, unroll=8)


def field_step(faces, scales, window_ops, window_pot, vector=None, local_in=None,
               received=None, older=None, alpha=1.0, apply=True):
    combine = local_in is not None
    has_older = older is not None
    node_total, cols = (local_in if combine else vector).shape
    face_total = faces.shape[0]
    cells, width, _ = window_ops.shape
    smem = pl.BlockSpec(memory_space=pltpu.SMEM)
    whole = pl.BlockSpec(memory_space=pltpu.VMEM)
    args, specs = [faces], [smem]
    if apply:
        args.append(scales); specs.append(smem)
    if combine:
        args += [local_in, received]; specs += [whole, whole]
        if has_older:
            args.append(older); specs.append(whole)
    else:
        args.append(vector); specs.append(whole)
    if apply:
        args += [window_ops, window_pot]
        specs += [pl.BlockSpec((1, width, width), lambda c: (c, 0, 0)),
                  pl.BlockSpec((1, width, cols), lambda c: (c, 0, 0))]
    out_shape, out_specs = [], []
    if combine:
        out_shape.append(jax.ShapeDtypeStruct((node_total, cols), jnp.bfloat16)); out_specs.append(whole)
    if apply:
        out_shape += [jax.ShapeDtypeStruct((node_total, cols), jnp.float32),
                      jax.ShapeDtypeStruct((face_total, cols), jnp.float32)]
        out_specs += [whole, whole]
    scratch = [pltpu.VMEM((node_total, cols), jnp.float32)] if combine else []
    flops = 2 * cells * width * width * cols if apply else 0
    result = pl.pallas_call(
        functools.partial(field_kernel, combine, has_older, apply, alpha),
        grid=(cells if apply else 1,),
        in_specs=specs,
        out_specs=out_specs,
        out_shape=out_shape,
        scratch_shapes=scratch,
        compiler_params=pltpu.CompilerParams(
            dimension_semantics=("arbitrary",), vmem_limit_bytes=VMEM_LIMIT),
        cost_estimate=pl.CostEstimate(
            flops=flops, transcendentals=0,
            bytes_accessed=(cells * width * width * 2 if apply else 0) + node_total * cols * 12),
    )(*args)
    return result


def operator_kernel(slot_ref, pot_ref, kinetic_ref, ops_ref, pot_out_ref):
    width = kinetic_ref.shape[0]
    cols = pot_out_ref.shape[2]
    slot_row = slot_ref[0]
    picks = (lax.broadcasted_iota(jnp.int32, (width, width), 0) == slot_row).astype(jnp.bfloat16)
    kinetic = kinetic_ref[...]
    columns = lax.dot_general(
        kinetic, picks, (((1,), (1,)), ((), ())), preferred_element_type=jnp.float32
    ).astype(jnp.bfloat16)
    ops_ref[0] = jnp.dot(picks, columns, preferred_element_type=jnp.float32).astype(ops_ref.dtype)
    pot_row = pot_ref[0]
    high = pot_row.astype(jnp.bfloat16)
    rest = pot_row - high.astype(jnp.float32)
    middle = rest.astype(jnp.bfloat16)
    low = (rest - middle.astype(jnp.float32)).astype(jnp.bfloat16)
    parts = jnp.concatenate(
        [high, middle, low, jnp.zeros((5, width), jnp.bfloat16)], axis=0
    )
    moved = lax.dot_general(
        parts, picks, (((1,), (1,)), ((), ())), preferred_element_type=jnp.float32
    )
    total = moved[0:1] + moved[1:2] + moved[2:3]
    column = jnp.transpose(jnp.broadcast_to(total, (8, width)))[:, 0:1]
    pot_out_ref[0] = jnp.broadcast_to(column, (width, cols))


def cell_operators(slots, potential, kinetic, cols):
    cells, width = slots.shape
    return pl.pallas_call(
        operator_kernel,
        grid=(cells,),
        in_specs=[
            pl.BlockSpec((1, 1, width), lambda c: (c, 0, 0)),
            pl.BlockSpec((1, 1, width), lambda c: (c, 0, 0)),
            pl.BlockSpec(memory_space=pltpu.VMEM),
        ],
        out_specs=[
            pl.BlockSpec((1, width, width), lambda c: (c, 0, 0)),
            pl.BlockSpec((1, width, cols), lambda c: (c, 0, 0)),
        ],
        out_shape=[
            jax.ShapeDtypeStruct((cells, width, width), jnp.bfloat16),
            jax.ShapeDtypeStruct((cells, width, cols), jnp.float32),
        ],
        compiler_params=pltpu.CompilerParams(dimension_semantics=("arbitrary",)),
        cost_estimate=pl.CostEstimate(
            flops=4 * cells * width * width * width, transcendentals=0,
            bytes_accessed=cells * width * (width * 2 + cols * 4 + 8)),
    )(slots.reshape(cells, 1, width), potential.reshape(cells, 1, width), kinetic)


def newton(gram_matrix):
    identity = jnp.eye(gram_matrix.shape[0], dtype=jnp.float32)
    frobenius = jnp.sqrt(jnp.sum(gram_matrix * gram_matrix))
    scaled = gram_matrix / frobenius
    inverse_root = identity
    for repeat in range(NS_ITERS):
        factor = 1.5 * identity - 0.5 * jnp.dot(
            inverse_root, scaled, precision=lax.Precision.HIGHEST
        )
        scaled = jnp.dot(scaled, factor, precision=lax.Precision.HIGHEST)
        inverse_root = jnp.dot(factor, inverse_root, precision=lax.Precision.HIGHEST)
    return inverse_root.astype(jnp.bfloat16)


def doubling_sum(value):
    band_size = lax.axis_size("band")
    count = lax.axis_size("dom") * band_size
    bits = list(range(count.bit_length() - 1))
    order = bits[2:3] + bits[0:2] + bits[3:]
    total = value
    for bit in order:
        mask = 1 << bit
        pairs = [(i, i ^ mask) for i in range(count)]
        total = total + lax.ppermute(total, ("dom", "band"), pairs)
    return total


def body(states, cell_kinetic, cell_scale, cell_potential, connectivity, shared_nodes, cell_counts):
    left_face = shared_nodes[0, 0]
    right_face = shared_nodes[0, 1]
    face_width = left_face.shape[0]
    faces = jnp.concatenate([left_face, right_face])
    live_count = cell_counts[0]
    domain = lax.axis_index("dom")
    domains = lax.axis_size("dom")
    node_total = states.shape[1]
    state_cols = states.shape[0]
    has_left = (domain > 0).astype(jnp.float32)
    has_right = (domain < domains - 1).astype(jnp.float32)
    multiplicity = (
        jnp.ones((node_total,), jnp.float32)
        .at[left_face]
        .add(has_left)
        .at[right_face]
        .add(has_right)
    )
    node_weight = (1.0 / multiplicity).astype(jnp.bfloat16)
    cells, width = connectivity.shape
    starts = jnp.arange(cells, dtype=jnp.int32) * (3 * (width // 4))
    slots = (connectivity - starts[:, None]) % node_total
    alive = (jnp.arange(cells) < live_count).astype(jnp.float32)
    scales = cell_scale * alive
    window_ops, window_pot = cell_operators(
        slots, cell_potential * alive[:, None], cell_kinetic, state_cols
    )
    up = [(i, i + 1) for i in range(domains - 1)]
    down = [(j, i) for i, j in up]

    def exchange(face_values):
        from_left = lax.ppermute(face_values[face_width:], "dom", up)
        from_right = lax.ppermute(face_values[:face_width], "dom", down)
        return jnp.concatenate([from_left, from_right], axis=0)

    step = functools.partial(field_step, faces, scales, window_ops, window_pot)
    first = states.T
    local_sum, face_values = step(vector=first)
    second, local_sum, face_values = step(local_in=local_sum, received=exchange(face_values))
    history = [first, second]
    for repeat in range(CHEB - 2):
        following, local_sum, face_values = step(
            local_in=local_sum, received=exchange(face_values), older=history[-2], alpha=2.0
        )
        history.append(following)
    (current,) = step(
        local_in=local_sum, received=exchange(face_values), older=history[-2], alpha=2.0,
        apply=False,
    )
    row_shard = lax.all_to_all(current, "band", split_axis=0, concat_axis=1, tiled=True)
    piece_nodes = row_shard.shape[0]
    weight_rows = lax.dynamic_slice_in_dim(
        node_weight, lax.axis_index("band") * piece_nodes, piece_nodes, 0
    )
    weighted = row_shard * weight_rows[:, None]
    partial_gram = lax.dot_general(
        weighted, row_shard, (((0,), (0,)), ((), ())), preferred_element_type=jnp.float32
    )
    gram_matrix = doubling_sum(partial_gram)
    mixing = newton(gram_matrix)
    rotated = lax.dot_general(
        row_shard, mixing, (((1,), (0,)), ((), ())), preferred_element_type=jnp.float32
    ).astype(jnp.bfloat16)
    back = lax.all_to_all(rotated, "band", split_axis=1, concat_axis=0, tiled=True)
    return back.T


def solution(mesh):
    in_specs = (
        P("band", "dom"),
        P(),
        P("dom"),
        P("dom", None),
        P("dom", None),
        P("dom", None, None),
        P("dom"),
    )
    out_specs = P("band", "dom")
    return jax.shard_map(body, mesh=mesh, in_specs=in_specs, out_specs=out_specs, check_vma=False)
```

```python
import functools

import jax
import jax.numpy as jnp
from jax import lax
from jax.experimental import pallas as pl
from jax.experimental.pallas import tpu as pltpu
from jax.sharding import PartitionSpec as P

CHEB = 4
NS_ITERS = 5


VMEM_LIMIT = 60 * 1024 * 1024


def field_kernel(combine, older, apply, alpha, *refs):
    refs = list(refs)
    faces = refs.pop(0)
    if apply:
        scales = refs.pop(0)
    if combine:
        local_in = refs.pop(0)
        received = refs.pop(0)
        if older:
            older_ref = refs.pop(0)
    else:
        vector_in = refs.pop(0)
    if apply:
        ops_ref = refs.pop(0)
        pot_ref = refs.pop(0)
    if combine:
        vector_out = refs.pop(0)
    if apply:
        local_out = refs.pop(0)
        faces_out = refs.pop(0)
    if combine:
        work = refs.pop(0)
    vector = vector_out if combine else vector_in
    face_total = faces.shape[0]
    node_total = vector.shape[0]
    cell = pl.program_id(0) if apply else None

    def prologue():
        work[...] = local_in[...] if alpha == 1.0 else alpha * local_in[...]

        def fix(p, carry):
            n = faces[p]
            row = received[pl.ds(p, 1), :]
            work[pl.ds(n, 1), :] += row if alpha == 1.0 else alpha * row
            return carry

        lax.fori_loop(0, face_total, fix, 0, unroll=8)
        value = work[...]
        if older:
            value = value - older_ref[...].astype(jnp.float32)
        vector_out[...] = value.astype(vector_out.dtype)

    if combine:
        if apply:
            pl.when(cell == 0)(prologue)
        else:
            prologue()

    if apply:
        width = ops_ref.shape[1]
        quarter = width // 4
        body_rows = width - quarter

        @pl.when(cell == 0)
        def _():
            local_out[...] = jnp.zeros_like(local_out)

        start = pl.multiple_of(cell * body_rows, quarter)
        tail = pl.multiple_of(lax.rem((cell + 1) * body_rows, node_total), quarter)
        main_rows = vector[pl.ds(start, body_rows), :]
        tail_rows = vector[pl.ds(tail, quarter), :]
        ops = ops_ref[0]
        product = jnp.dot(ops[:, :body_rows], main_rows, preferred_element_type=jnp.float32)
        product = product + jnp.dot(ops[:, body_rows:], tail_rows, preferred_element_type=jnp.float32)
        scale = scales[cell]
        pot = pot_ref[0]
        top = product[:body_rows] * scale + pot[:body_rows] * main_rows.astype(jnp.float32)
        bottom = product[body_rows:] * scale + pot[body_rows:] * tail_rows.astype(jnp.float32)
        local_out[pl.ds(start, body_rows), :] += top
        local_out[pl.ds(tail, quarter), :] += bottom

        @pl.when(cell == pl.num_programs(0) - 1)
        def _():
            def pick(p, carry):
                n = faces[p]
                faces_out[pl.ds(p, 1), :] = local_out[pl.ds(n, 1), :]
                return carry

            lax.fori_loop(0, face_total, pick, 0, unroll=8)


def field_step(faces, scales, window_ops, window_pot, vector=None, local_in=None,
               received=None, older=None, alpha=1.0, apply=True):
    combine = local_in is not None
    has_older = older is not None
    node_total, cols = (local_in if combine else vector).shape
    face_total = faces.shape[0]
    cells, width, _ = window_ops.shape
    smem = pl.BlockSpec(memory_space=pltpu.SMEM)
    whole = pl.BlockSpec(memory_space=pltpu.VMEM)
    args, specs = [faces], [smem]
    if apply:
        args.append(scales); specs.append(smem)
    if combine:
        args += [local_in, received]; specs += [whole, whole]
        if has_older:
            args.append(older); specs.append(whole)
    else:
        args.append(vector); specs.append(whole)
    if apply:
        args += [window_ops, window_pot]
        specs += [pl.BlockSpec((1, width, width), lambda c: (c, 0, 0)),
                  pl.BlockSpec((1, width, cols), lambda c: (c, 0, 0))]
    out_shape, out_specs = [], []
    if combine:
        out_shape.append(jax.ShapeDtypeStruct((node_total, cols), jnp.bfloat16)); out_specs.append(whole)
    if apply:
        out_shape += [jax.ShapeDtypeStruct((node_total, cols), jnp.float32),
                      jax.ShapeDtypeStruct((face_total, cols), jnp.float32)]
        out_specs += [whole, whole]
    scratch = [pltpu.VMEM((node_total, cols), jnp.float32)] if combine else []
    flops = 2 * cells * width * width * cols if apply else 0
    result = pl.pallas_call(
        functools.partial(field_kernel, combine, has_older, apply, alpha),
        grid=(cells if apply else 1,),
        in_specs=specs,
        out_specs=out_specs,
        out_shape=out_shape,
        scratch_shapes=scratch,
        compiler_params=pltpu.CompilerParams(
            dimension_semantics=("arbitrary",), vmem_limit_bytes=VMEM_LIMIT),
        cost_estimate=pl.CostEstimate(
            flops=flops, transcendentals=0,
            bytes_accessed=(cells * width * width * 2 if apply else 0) + node_total * cols * 12),
    )(*args)
    return result


def operator_kernel(slot_ref, pot_ref, kinetic_ref, ops_ref, pot_out_ref):
    width = kinetic_ref.shape[0]
    cols = pot_out_ref.shape[2]
    slot_row = slot_ref[0]
    slot_column = jnp.transpose(jnp.broadcast_to(slot_row, (8, width)))[:, 0:1]
    picks = (lax.broadcasted_iota(jnp.int32, (width, width), 1) == slot_column).astype(jnp.bfloat16)
    picks_t = (lax.broadcasted_iota(jnp.int32, (width, width), 0) == slot_row).astype(jnp.bfloat16)
    columns = jnp.dot(kinetic_ref[...], picks, preferred_element_type=jnp.float32).astype(jnp.bfloat16)
    ops_ref[0] = jnp.dot(picks_t, columns, preferred_element_type=jnp.float32).astype(ops_ref.dtype)
    pot_row = pot_ref[0]
    high = pot_row.astype(jnp.bfloat16)
    rest = pot_row - high.astype(jnp.float32)
    middle = rest.astype(jnp.bfloat16)
    low = (rest - middle.astype(jnp.float32)).astype(jnp.bfloat16)
    parts = jnp.concatenate(
        [high, middle, low, jnp.zeros((5, width), jnp.bfloat16)], axis=0
    )
    moved = jnp.dot(parts, picks, preferred_element_type=jnp.float32)
    total = moved[0:1] + moved[1:2] + moved[2:3]
    column = jnp.transpose(jnp.broadcast_to(total, (8, width)))[:, 0:1]
    pot_out_ref[0] = jnp.broadcast_to(column, (width, cols))


def cell_operators(slots, potential, kinetic, cols):
    cells, width = slots.shape
    return pl.pallas_call(
        operator_kernel,
        grid=(cells,),
        in_specs=[
            pl.BlockSpec((1, 1, width), lambda c: (c, 0, 0)),
            pl.BlockSpec((1, 1, width), lambda c: (c, 0, 0)),
            pl.BlockSpec(memory_space=pltpu.VMEM),
        ],
        out_specs=[
            pl.BlockSpec((1, width, width), lambda c: (c, 0, 0)),
            pl.BlockSpec((1, width, cols), lambda c: (c, 0, 0)),
        ],
        out_shape=[
            jax.ShapeDtypeStruct((cells, width, width), jnp.bfloat16),
            jax.ShapeDtypeStruct((cells, width, cols), jnp.float32),
        ],
        compiler_params=pltpu.CompilerParams(dimension_semantics=("arbitrary",)),
        cost_estimate=pl.CostEstimate(
            flops=4 * cells * width * width * width, transcendentals=0,
            bytes_accessed=cells * width * (width * 2 + cols * 4 + 8)),
    )(slots.reshape(cells, 1, width), potential.reshape(cells, 1, width), kinetic)


def newton(gram_matrix):
    identity = jnp.eye(gram_matrix.shape[0], dtype=jnp.float32)
    frobenius = jnp.sqrt(jnp.sum(gram_matrix * gram_matrix))
    scaled = gram_matrix / frobenius
    inverse_root = identity
    for repeat in range(NS_ITERS):
        factor = 1.5 * identity - 0.5 * jnp.dot(
            inverse_root, scaled, precision=lax.Precision.HIGHEST
        )
        scaled = jnp.dot(scaled, factor, precision=lax.Precision.HIGHEST)
        inverse_root = jnp.dot(factor, inverse_root, precision=lax.Precision.HIGHEST)
    return inverse_root.astype(jnp.bfloat16)


def doubling_sum(value):
    band_size = lax.axis_size("band")
    count = lax.axis_size("dom") * band_size
    bits = list(range(count.bit_length() - 1))
    order = bits[2:3] + bits[0:2] + bits[3:]
    total = value
    for bit in order:
        mask = 1 << bit
        pairs = [(i, i ^ mask) for i in range(count)]
        total = total + lax.ppermute(total, ("dom", "band"), pairs)
    return total


def body(states, cell_kinetic, cell_scale, cell_potential, connectivity, shared_nodes, cell_counts):
    left_face = shared_nodes[0, 0]
    right_face = shared_nodes[0, 1]
    face_width = left_face.shape[0]
    faces = jnp.concatenate([left_face, right_face])
    live_count = cell_counts[0]
    domain = lax.axis_index("dom")
    domains = lax.axis_size("dom")
    node_total = states.shape[1]
    state_cols = states.shape[0]
    has_left = (domain > 0).astype(jnp.float32)
    has_right = (domain < domains - 1).astype(jnp.float32)
    face_counts = jnp.concatenate(
        [jnp.full((face_width,), has_left), jnp.full((face_width,), has_right)]
    )
    node_weight = (
        jnp.ones((node_total,), jnp.float32)
        .at[faces]
        .set(1.0 / (1.0 + face_counts), unique_indices=True)
        .astype(jnp.bfloat16)
    )
    cells, width = connectivity.shape
    starts = jnp.arange(cells, dtype=jnp.int32) * (3 * (width // 4))
    slots = (connectivity - starts[:, None]) % node_total
    alive = (jnp.arange(cells) < live_count).astype(jnp.float32)
    scales = cell_scale * alive
    window_ops, window_pot = cell_operators(
        slots, cell_potential * alive[:, None], cell_kinetic, state_cols
    )
    up = [(i, i + 1) for i in range(domains - 1)]
    down = [(j, i) for i, j in up]

    def exchange(face_values):
        from_left = lax.ppermute(face_values[face_width:], "dom", up)
        from_right = lax.ppermute(face_values[:face_width], "dom", down)
        return jnp.concatenate([from_left, from_right], axis=0)

    step = functools.partial(field_step, faces, scales, window_ops, window_pot)
    first = states.T
    local_sum, face_values = step(vector=first)
    second, local_sum, face_values = step(local_in=local_sum, received=exchange(face_values))
    history = [first, second]
    for repeat in range(CHEB - 2):
        following, local_sum, face_values = step(
            local_in=local_sum, received=exchange(face_values), older=history[-2], alpha=2.0
        )
        history.append(following)
    (current,) = step(
        local_in=local_sum, received=exchange(face_values), older=history[-2], alpha=2.0,
        apply=False,
    )
    row_shard = lax.all_to_all(current, "band", split_axis=0, concat_axis=1, tiled=True)
    piece_nodes = row_shard.shape[0]
    weight_rows = lax.dynamic_slice_in_dim(
        node_weight, lax.axis_index("band") * piece_nodes, piece_nodes, 0
    )
    weighted = row_shard * weight_rows[:, None]
    partial_gram = lax.dot_general(
        weighted, row_shard, (((0,), (0,)), ((), ())), preferred_element_type=jnp.float32
    )
    gram_matrix = doubling_sum(partial_gram)
    mixing = newton(gram_matrix)
    rotated = lax.dot_general(
        row_shard, mixing, (((1,), (0,)), ((), ())), preferred_element_type=jnp.float32
    ).astype(jnp.bfloat16)
    back = lax.all_to_all(rotated, "band", split_axis=1, concat_axis=0, tiled=True)
    return back.T


def solution(mesh):
    in_specs = (
        P("band", "dom"),
        P(),
        P("dom"),
        P("dom", None),
        P("dom", None),
        P("dom", None, None),
        P("dom"),
    )
    out_specs = P("band", "dom")
    return jax.shard_map(body, mesh=mesh, in_specs=in_specs, out_specs=out_specs, check_vma=False)
```

```python
import functools

import jax
import jax.numpy as jnp
from jax import lax
from jax.experimental import pallas as pl
from jax.experimental.pallas import tpu as pltpu
from jax.sharding import PartitionSpec as P

CHEB = 4
NS_ITERS = 5


VMEM_LIMIT = 60 * 1024 * 1024


def field_kernel(combine, older, apply, alpha, *refs):
    refs = list(refs)
    faces = refs.pop(0)
    if apply:
        scales = refs.pop(0)
    if combine:
        local_in = refs.pop(0)
        received = refs.pop(0)
        if older:
            older_ref = refs.pop(0)
    else:
        vector_in = refs.pop(0)
    if apply:
        ops_ref = refs.pop(0)
        pot_ref = refs.pop(0)
    if combine:
        vector_out = refs.pop(0)
    if apply:
        local_out = refs.pop(0)
        faces_out = refs.pop(0)
    if combine:
        work = refs.pop(0)
    vector = vector_out if combine else vector_in
    face_total = faces.shape[0]
    node_total = vector.shape[0]
    cell = pl.program_id(0) if apply else None

    def prologue():
        work[...] = local_in[...] if alpha == 1.0 else alpha * local_in[...]

        def fix(p, carry):
            n = faces[p]
            row = received[pl.ds(p, 1), :]
            work[pl.ds(n, 1), :] += row if alpha == 1.0 else alpha * row
            return carry

        lax.fori_loop(0, face_total, fix, 0, unroll=8)
        value = work[...]
        if older:
            value = value - older_ref[...].astype(jnp.float32)
        vector_out[...] = value.astype(vector_out.dtype)

    if combine:
        if apply:
            pl.when(cell == 0)(prologue)
        else:
            prologue()

    if apply:
        width = ops_ref.shape[1]
        quarter = width // 4
        body_rows = width - quarter

        @pl.when(cell == 0)
        def _():
            local_out[...] = jnp.zeros_like(local_out)

        start = pl.multiple_of(cell * body_rows, quarter)
        tail = pl.multiple_of(lax.rem((cell + 1) * body_rows, node_total), quarter)
        main_rows = vector[pl.ds(start, body_rows), :]
        tail_rows = vector[pl.ds(tail, quarter), :]
        ops = ops_ref[0]
        product = jnp.dot(ops[:, :body_rows], main_rows, preferred_element_type=jnp.float32)
        product = product + jnp.dot(ops[:, body_rows:], tail_rows, preferred_element_type=jnp.float32)
        scale = scales[cell]
        pot = jnp.transpose(jnp.broadcast_to(pot_ref[0], (8, width)))[:, 0:1]
        top = product[:body_rows] * scale + pot[:body_rows] * main_rows.astype(jnp.float32)
        bottom = product[body_rows:] * scale + pot[body_rows:] * tail_rows.astype(jnp.float32)
        local_out[pl.ds(start, body_rows), :] += top
        local_out[pl.ds(tail, quarter), :] += bottom

        @pl.when(cell == pl.num_programs(0) - 1)
        def _():
            def pick(p, carry):
                n = faces[p]
                faces_out[pl.ds(p, 1), :] = local_out[pl.ds(n, 1), :]
                return carry

            lax.fori_loop(0, face_total, pick, 0, unroll=8)


def field_step(faces, scales, window_ops, window_pot, vector=None, local_in=None,
               received=None, older=None, alpha=1.0, apply=True):
    combine = local_in is not None
    has_older = older is not None
    node_total, cols = (local_in if combine else vector).shape
    face_total = faces.shape[0]
    cells, width, _ = window_ops.shape
    smem = pl.BlockSpec(memory_space=pltpu.SMEM)
    whole = pl.BlockSpec(memory_space=pltpu.VMEM)
    args, specs = [faces], [smem]
    if apply:
        args.append(scales); specs.append(smem)
    if combine:
        args += [local_in, received]; specs += [whole, whole]
        if has_older:
            args.append(older); specs.append(whole)
    else:
        args.append(vector); specs.append(whole)
    if apply:
        args += [window_ops, window_pot]
        specs += [pl.BlockSpec((1, width, width), lambda c: (c, 0, 0)),
                  pl.BlockSpec((1, 1, width), lambda c: (c, 0, 0))]
    out_shape, out_specs = [], []
    if combine:
        out_shape.append(jax.ShapeDtypeStruct((node_total, cols), jnp.bfloat16)); out_specs.append(whole)
    if apply:
        out_shape += [jax.ShapeDtypeStruct((node_total, cols), jnp.float32),
                      jax.ShapeDtypeStruct((face_total, cols), jnp.float32)]
        out_specs += [whole, whole]
    scratch = [pltpu.VMEM((node_total, cols), jnp.float32)] if combine else []
    flops = 2 * cells * width * width * cols if apply else 0
    result = pl.pallas_call(
        functools.partial(field_kernel, combine, has_older, apply, alpha),
        grid=(cells if apply else 1,),
        in_specs=specs,
        out_specs=out_specs,
        out_shape=out_shape,
        scratch_shapes=scratch,
        compiler_params=pltpu.CompilerParams(
            dimension_semantics=("arbitrary",), vmem_limit_bytes=VMEM_LIMIT),
        cost_estimate=pl.CostEstimate(
            flops=flops, transcendentals=0,
            bytes_accessed=(cells * width * width * 2 if apply else 0) + node_total * cols * 12),
    )(*args)
    return result


def operator_kernel(slot_ref, pot_ref, kinetic_ref, ops_ref, pot_out_ref):
    width = kinetic_ref.shape[0]
    slot_row = slot_ref[0]
    picks = (lax.broadcasted_iota(jnp.int32, (width, width), 0) == slot_row).astype(jnp.bfloat16)
    kinetic = kinetic_ref[...]
    columns = lax.dot_general(
        kinetic, picks, (((1,), (1,)), ((), ())), preferred_element_type=jnp.float32
    ).astype(jnp.bfloat16)
    ops_ref[0] = jnp.dot(picks, columns, preferred_element_type=jnp.float32).astype(ops_ref.dtype)
    pot_row = pot_ref[0]
    high = pot_row.astype(jnp.bfloat16)
    rest = pot_row - high.astype(jnp.float32)
    middle = rest.astype(jnp.bfloat16)
    low = (rest - middle.astype(jnp.float32)).astype(jnp.bfloat16)
    parts = jnp.concatenate(
        [high, middle, low, jnp.zeros((5, width), jnp.bfloat16)], axis=0
    )
    moved = lax.dot_general(
        parts, picks, (((1,), (1,)), ((), ())), preferred_element_type=jnp.float32
    )
    pot_out_ref[0] = moved[0:1] + moved[1:2] + moved[2:3]


def cell_operators(slots, potential, kinetic, cols):
    cells, width = slots.shape
    return pl.pallas_call(
        operator_kernel,
        grid=(cells,),
        in_specs=[
            pl.BlockSpec((1, 1, width), lambda c: (c, 0, 0)),
            pl.BlockSpec((1, 1, width), lambda c: (c, 0, 0)),
            pl.BlockSpec(memory_space=pltpu.VMEM),
        ],
        out_specs=[
            pl.BlockSpec((1, width, width), lambda c: (c, 0, 0)),
            pl.BlockSpec((1, 1, width), lambda c: (c, 0, 0)),
        ],
        out_shape=[
            jax.ShapeDtypeStruct((cells, width, width), jnp.bfloat16),
            jax.ShapeDtypeStruct((cells, 1, width), jnp.float32),
        ],
        compiler_params=pltpu.CompilerParams(dimension_semantics=("arbitrary",)),
        cost_estimate=pl.CostEstimate(
            flops=4 * cells * width * width * width, transcendentals=0,
            bytes_accessed=cells * width * (width * 2 + 12)),
    )(slots.reshape(cells, 1, width), potential.reshape(cells, 1, width), kinetic)


def newton(gram_matrix):
    identity = jnp.eye(gram_matrix.shape[0], dtype=jnp.float32)
    frobenius = jnp.sqrt(jnp.sum(gram_matrix * gram_matrix))
    scaled = gram_matrix / frobenius
    inverse_root = identity
    for repeat in range(NS_ITERS):
        factor = 1.5 * identity - 0.5 * jnp.dot(
            inverse_root, scaled, precision=lax.Precision.HIGHEST
        )
        scaled = jnp.dot(scaled, factor, precision=lax.Precision.HIGHEST)
        inverse_root = jnp.dot(factor, inverse_root, precision=lax.Precision.HIGHEST)
    return inverse_root.astype(jnp.bfloat16)


def doubling_sum(value):
    band_size = lax.axis_size("band")
    count = lax.axis_size("dom") * band_size
    bits = list(range(count.bit_length() - 1))
    order = bits[2:3] + bits[0:2] + bits[3:]
    total = value
    for bit in order:
        mask = 1 << bit
        pairs = [(i, i ^ mask) for i in range(count)]
        total = total + lax.ppermute(total, ("dom", "band"), pairs)
    return total


def body(states, cell_kinetic, cell_scale, cell_potential, connectivity, shared_nodes, cell_counts):
    left_face = shared_nodes[0, 0]
    right_face = shared_nodes[0, 1]
    face_width = left_face.shape[0]
    faces = jnp.concatenate([left_face, right_face])
    live_count = cell_counts[0]
    domain = lax.axis_index("dom")
    domains = lax.axis_size("dom")
    node_total = states.shape[1]
    state_cols = states.shape[0]
    has_left = (domain > 0).astype(jnp.float32)
    has_right = (domain < domains - 1).astype(jnp.float32)
    face_counts = jnp.concatenate(
        [jnp.full((face_width,), has_left), jnp.full((face_width,), has_right)]
    )
    node_weight = (
        jnp.ones((node_total,), jnp.float32)
        .at[faces]
        .set(1.0 / (1.0 + face_counts), unique_indices=True)
        .astype(jnp.bfloat16)
    )
    cells, width = connectivity.shape
    starts = jnp.arange(cells, dtype=jnp.int32) * (3 * (width // 4))
    slots = (connectivity - starts[:, None]) % node_total
    alive = (jnp.arange(cells) < live_count).astype(jnp.float32)
    scales = cell_scale * alive
    window_ops, window_pot = cell_operators(
        slots, cell_potential * alive[:, None], cell_kinetic, state_cols
    )
    up = [(i, i + 1) for i in range(domains - 1)]
    down = [(j, i) for i, j in up]

    def exchange(face_values):
        from_left = lax.ppermute(face_values[face_width:], "dom", up)
        from_right = lax.ppermute(face_values[:face_width], "dom", down)
        return jnp.concatenate([from_left, from_right], axis=0)

    step = functools.partial(field_step, faces, scales, window_ops, window_pot)
    first = states.T
    local_sum, face_values = step(vector=first)
    second, local_sum, face_values = step(local_in=local_sum, received=exchange(face_values))
    history = [first, second]
    for repeat in range(CHEB - 2):
        following, local_sum, face_values = step(
            local_in=local_sum, received=exchange(face_values), older=history[-2], alpha=2.0
        )
        history.append(following)
    (current,) = step(
        local_in=local_sum, received=exchange(face_values), older=history[-2], alpha=2.0,
        apply=False,
    )
    row_shard = lax.all_to_all(current, "band", split_axis=0, concat_axis=1, tiled=True)
    piece_nodes = row_shard.shape[0]
    weight_rows = lax.dynamic_slice_in_dim(
        node_weight, lax.axis_index("band") * piece_nodes, piece_nodes, 0
    )
    weighted = row_shard * weight_rows[:, None]
    partial_gram = lax.dot_general(
        weighted, row_shard, (((0,), (0,)), ((), ())), preferred_element_type=jnp.float32
    )
    gram_matrix = doubling_sum(partial_gram)
    mixing = newton(gram_matrix)
    rotated = lax.dot_general(
        row_shard, mixing, (((1,), (0,)), ((), ())), preferred_element_type=jnp.float32
    ).astype(jnp.bfloat16)
    back = lax.all_to_all(rotated, "band", split_axis=1, concat_axis=0, tiled=True)
    return back.T


def solution(mesh):
    in_specs = (
        P("band", "dom"),
        P(),
        P("dom"),
        P("dom", None),
        P("dom", None),
        P("dom", None, None),
        P("dom"),
    )
    out_specs = P("band", "dom")
    return jax.shard_map(body, mesh=mesh, in_specs=in_specs, out_specs=out_specs, check_vma=False)
```

```python
import functools

import jax
import jax.numpy as jnp
from jax import lax
from jax.experimental import pallas as pl
from jax.experimental.pallas import tpu as pltpu
from jax.sharding import PartitionSpec as P

CHEB = 4
NS_ITERS = 5


VMEM_LIMIT = 60 * 1024 * 1024


def field_kernel(combine, older, apply, build, alpha, *refs):
    refs = list(refs)
    faces = refs.pop(0)
    if apply:
        scales = refs.pop(0)
    if combine:
        local_in = refs.pop(0)
        received = refs.pop(0)
        if older:
            older_ref = refs.pop(0)
    else:
        vector_in = refs.pop(0)
    if apply:
        ops_ref = refs.pop(0)
        pot_ref = refs.pop(0)
        if build:
            kinetic_ref = refs.pop(0)
    if combine:
        vector_out = refs.pop(0)
    if apply:
        local_out = refs.pop(0)
        faces_out = refs.pop(0)
        if build:
            ops_out = refs.pop(0)
            pot_out = refs.pop(0)
    if combine:
        work = refs.pop(0)
    vector = vector_out if combine else vector_in
    face_total = faces.shape[0]
    node_total = vector.shape[0]
    cell = pl.program_id(0) if apply else None

    def prologue():
        work[...] = local_in[...] if alpha == 1.0 else alpha * local_in[...]

        def fix(p, carry):
            n = faces[p]
            row = received[pl.ds(p, 1), :]
            work[pl.ds(n, 1), :] += row if alpha == 1.0 else alpha * row
            return carry

        lax.fori_loop(0, face_total, fix, 0, unroll=8)
        value = work[...]
        if older:
            value = value - older_ref[...].astype(jnp.float32)
        vector_out[...] = value.astype(vector_out.dtype)

    if combine:
        if apply:
            pl.when(cell == 0)(prologue)
        else:
            prologue()

    if apply:
        width = ops_ref.shape[-1]
        quarter = width // 4
        body_rows = width - quarter

        @pl.when(cell == 0)
        def _():
            local_out[...] = jnp.zeros_like(local_out)

        start = pl.multiple_of(cell * body_rows, quarter)
        tail = pl.multiple_of(lax.rem((cell + 1) * body_rows, node_total), quarter)
        main_rows = vector[pl.ds(start, body_rows), :]
        tail_rows = vector[pl.ds(tail, quarter), :]
        if build:
            ops, pot_row = build_operator(ops_ref[0], pot_ref[0], kinetic_ref[...])
            ops_out[0] = ops
            pot_out[0] = pot_row
        else:
            ops = ops_ref[0]
            pot_row = pot_ref[0]
        product = jnp.dot(ops[:, :body_rows], main_rows, preferred_element_type=jnp.float32)
        product = product + jnp.dot(ops[:, body_rows:], tail_rows, preferred_element_type=jnp.float32)
        scale = scales[cell]
        pot = jnp.transpose(jnp.broadcast_to(pot_row, (8, width)))[:, 0:1]
        top = product[:body_rows] * scale + pot[:body_rows] * main_rows.astype(jnp.float32)
        bottom = product[body_rows:] * scale + pot[body_rows:] * tail_rows.astype(jnp.float32)
        local_out[pl.ds(start, body_rows), :] += top
        local_out[pl.ds(tail, quarter), :] += bottom

        @pl.when(cell == pl.num_programs(0) - 1)
        def _():
            def pick(p, carry):
                n = faces[p]
                faces_out[pl.ds(p, 1), :] = local_out[pl.ds(n, 1), :]
                return carry

            lax.fori_loop(0, face_total, pick, 0, unroll=8)


def field_step(faces, scales, window_ops, window_pot, vector=None, local_in=None,
               received=None, older=None, alpha=1.0, apply=True, kinetic=None):
    combine = local_in is not None
    has_older = older is not None
    build = kinetic is not None
    node_total, cols = (local_in if combine else vector).shape
    face_total = faces.shape[0]
    cells, width = window_pot.shape[0], window_pot.shape[-1]
    smem = pl.BlockSpec(memory_space=pltpu.SMEM)
    whole = pl.BlockSpec(memory_space=pltpu.VMEM)
    args, specs = [faces], [smem]
    if apply:
        args.append(scales); specs.append(smem)
    if combine:
        args += [local_in, received]; specs += [whole, whole]
        if has_older:
            args.append(older); specs.append(whole)
    else:
        args.append(vector); specs.append(whole)
    cell_block = pl.BlockSpec((1, width, width), lambda c: (c, 0, 0))
    row_block = pl.BlockSpec((1, 1, width), lambda c: (c, 0, 0))
    if apply:
        args += [window_ops, window_pot]
        specs += [row_block if build else cell_block, row_block]
        if build:
            args.append(kinetic); specs.append(whole)
    out_shape, out_specs = [], []
    if combine:
        out_shape.append(jax.ShapeDtypeStruct((node_total, cols), jnp.bfloat16)); out_specs.append(whole)
    if apply:
        out_shape += [jax.ShapeDtypeStruct((node_total, cols), jnp.float32),
                      jax.ShapeDtypeStruct((face_total, cols), jnp.float32)]
        out_specs += [whole, whole]
        if build:
            out_shape += [jax.ShapeDtypeStruct((cells, width, width), jnp.bfloat16),
                          jax.ShapeDtypeStruct((cells, 1, width), jnp.float32)]
            out_specs += [cell_block, row_block]
    scratch = [pltpu.VMEM((node_total, cols), jnp.float32)] if combine else []
    flops = (2 * cells * width * width * cols if apply else 0) + (4 * cells * width ** 3 if build else 0)
    result = pl.pallas_call(
        functools.partial(field_kernel, combine, has_older, apply, build, alpha),
        grid=(cells if apply else 1,),
        in_specs=specs,
        out_specs=out_specs,
        out_shape=out_shape,
        scratch_shapes=scratch,
        compiler_params=pltpu.CompilerParams(
            dimension_semantics=("arbitrary",), vmem_limit_bytes=VMEM_LIMIT),
        cost_estimate=pl.CostEstimate(
            flops=flops, transcendentals=0,
            bytes_accessed=(cells * width * width * 2 if apply else 0) + node_total * cols * 12),
    )(*args)
    return result


def build_operator(slot_row, pot_row, kinetic):
    width = kinetic.shape[0]
    picks = (lax.broadcasted_iota(jnp.int32, (width, width), 0) == slot_row).astype(jnp.bfloat16)
    columns = lax.dot_general(
        kinetic, picks, (((1,), (1,)), ((), ())), preferred_element_type=jnp.float32
    ).astype(jnp.bfloat16)
    ops = jnp.dot(picks, columns, preferred_element_type=jnp.float32).astype(jnp.bfloat16)
    high = pot_row.astype(jnp.bfloat16)
    rest = pot_row - high.astype(jnp.float32)
    middle = rest.astype(jnp.bfloat16)
    low = (rest - middle.astype(jnp.float32)).astype(jnp.bfloat16)
    parts = jnp.concatenate(
        [high, middle, low, jnp.zeros((5, width), jnp.bfloat16)], axis=0
    )
    moved = lax.dot_general(
        parts, picks, (((1,), (1,)), ((), ())), preferred_element_type=jnp.float32
    )
    return ops, moved[0:1] + moved[1:2] + moved[2:3]


def newton(gram_matrix):
    identity = jnp.eye(gram_matrix.shape[0], dtype=jnp.float32)
    frobenius = jnp.sqrt(jnp.sum(gram_matrix * gram_matrix))
    scaled = gram_matrix / frobenius
    inverse_root = identity
    for repeat in range(NS_ITERS):
        factor = 1.5 * identity - 0.5 * jnp.dot(
            inverse_root, scaled, precision=lax.Precision.HIGHEST
        )
        scaled = jnp.dot(scaled, factor, precision=lax.Precision.HIGHEST)
        inverse_root = jnp.dot(factor, inverse_root, precision=lax.Precision.HIGHEST)
    return inverse_root.astype(jnp.bfloat16)


def doubling_sum(value):
    band_size = lax.axis_size("band")
    count = lax.axis_size("dom") * band_size
    bits = list(range(count.bit_length() - 1))
    order = bits[2:3] + bits[0:2] + bits[3:]
    total = value
    for bit in order:
        mask = 1 << bit
        pairs = [(i, i ^ mask) for i in range(count)]
        total = total + lax.ppermute(total, ("dom", "band"), pairs)
    return total


def body(states, cell_kinetic, cell_scale, cell_potential, connectivity, shared_nodes, cell_counts):
    left_face = shared_nodes[0, 0]
    right_face = shared_nodes[0, 1]
    face_width = left_face.shape[0]
    faces = jnp.concatenate([left_face, right_face])
    live_count = cell_counts[0]
    domain = lax.axis_index("dom")
    domains = lax.axis_size("dom")
    node_total = states.shape[1]
    state_cols = states.shape[0]
    has_left = (domain > 0).astype(jnp.float32)
    has_right = (domain < domains - 1).astype(jnp.float32)
    face_counts = jnp.concatenate(
        [jnp.full((face_width,), has_left), jnp.full((face_width,), has_right)]
    )
    node_weight = (
        jnp.ones((node_total,), jnp.float32)
        .at[faces]
        .set(1.0 / (1.0 + face_counts), unique_indices=True)
        .astype(jnp.bfloat16)
    )
    cells, width = connectivity.shape
    starts = jnp.arange(cells, dtype=jnp.int32) * (3 * (width // 4))
    slots = (connectivity - starts[:, None]) % node_total
    alive = (jnp.arange(cells) < live_count).astype(jnp.float32)
    scales = cell_scale * alive
    slot_rows = slots.reshape(cells, 1, width)
    potential_rows = (cell_potential * alive[:, None]).reshape(cells, 1, width)
    up = [(i, i + 1) for i in range(domains - 1)]
    down = [(j, i) for i, j in up]

    def exchange(face_values):
        from_left = lax.ppermute(face_values[face_width:], "dom", up)
        from_right = lax.ppermute(face_values[:face_width], "dom", down)
        return jnp.concatenate([from_left, from_right], axis=0)

    first = states.T
    local_sum, face_values, window_ops, window_pot = field_step(
        faces, scales, slot_rows, potential_rows, vector=first, kinetic=cell_kinetic
    )
    step = functools.partial(field_step, faces, scales, window_ops, window_pot)
    second, local_sum, face_values = step(local_in=local_sum, received=exchange(face_values))
    history = [first, second]
    for repeat in range(CHEB - 2):
        following, local_sum, face_values = step(
            local_in=local_sum, received=exchange(face_values), older=history[-2], alpha=2.0
        )
        history.append(following)
    (current,) = step(
        local_in=local_sum, received=exchange(face_values), older=history[-2], alpha=2.0,
        apply=False,
    )
    row_shard = lax.all_to_all(current, "band", split_axis=0, concat_axis=1, tiled=True)
    piece_nodes = row_shard.shape[0]
    weight_rows = lax.dynamic_slice_in_dim(
        node_weight, lax.axis_index("band") * piece_nodes, piece_nodes, 0
    )
    weighted = row_shard * weight_rows[:, None]
    partial_gram = lax.dot_general(
        weighted, row_shard, (((0,), (0,)), ((), ())), preferred_element_type=jnp.float32
    )
    gram_matrix = doubling_sum(partial_gram)
    mixing = newton(gram_matrix)
    rotated = lax.dot_general(
        row_shard, mixing, (((1,), (0,)), ((), ())), preferred_element_type=jnp.float32
    ).astype(jnp.bfloat16)
    back = lax.all_to_all(rotated, "band", split_axis=1, concat_axis=0, tiled=True)
    return back.T


def solution(mesh):
    in_specs = (
        P("band", "dom"),
        P(),
        P("dom"),
        P("dom", None),
        P("dom", None),
        P("dom", None, None),
        P("dom"),
    )
    out_specs = P("band", "dom")
    return jax.shard_map(body, mesh=mesh, in_specs=in_specs, out_specs=out_specs, check_vma=False)
```

```python
import functools

import jax
import jax.numpy as jnp
from jax import lax
from jax.experimental import pallas as pl
from jax.experimental.pallas import tpu as pltpu
from jax.sharding import PartitionSpec as P

CHEB = 4
NS_ITERS = 5


VMEM_LIMIT = 60 * 1024 * 1024


def field_kernel(combine, older, apply, build, alpha, *refs):
    refs = list(refs)
    faces = refs.pop(0)
    if apply:
        scales = refs.pop(0)
    if combine:
        local_in = refs.pop(0)
        received = (refs.pop(0), refs.pop(0))
        if older:
            older_ref = refs.pop(0)
    else:
        vector_in = refs.pop(0)
    if apply:
        ops_ref = refs.pop(0)
        pot_ref = refs.pop(0)
        if build:
            kinetic_ref = refs.pop(0)
    if combine:
        vector_out = refs.pop(0)
    if apply:
        local_out = refs.pop(0)
        faces_out = (refs.pop(0), refs.pop(0))
        if build:
            ops_out = refs.pop(0)
            pot_out = refs.pop(0)
    if combine:
        work = refs.pop(0)
    vector = vector_out if combine else vector_in
    face_half = faces.shape[0] // 2
    node_total = vector.shape[0]
    cell = pl.program_id(0) if apply else None

    def prologue():
        work[...] = local_in[...] if alpha == 1.0 else alpha * local_in[...]

        for side in range(2):
            def fix(p, carry):
                n = faces[side * face_half + p]
                row = received[side][pl.ds(p, 1), :]
                work[pl.ds(n, 1), :] += row if alpha == 1.0 else alpha * row
                return carry

            lax.fori_loop(0, face_half, fix, 0, unroll=8)
        value = work[...]
        if older:
            value = value - older_ref[...].astype(jnp.float32)
        vector_out[...] = value.astype(vector_out.dtype)

    if combine:
        if apply:
            pl.when(cell == 0)(prologue)
        else:
            prologue()

    if apply:
        width = ops_ref.shape[-1]
        quarter = width // 4
        body_rows = width - quarter

        @pl.when(cell == 0)
        def _():
            local_out[...] = jnp.zeros_like(local_out)

        start = pl.multiple_of(cell * body_rows, quarter)
        tail = pl.multiple_of(lax.rem((cell + 1) * body_rows, node_total), quarter)
        main_rows = vector[pl.ds(start, body_rows), :]
        tail_rows = vector[pl.ds(tail, quarter), :]
        if build:
            ops, pot_row = build_operator(ops_ref[0], pot_ref[0], kinetic_ref[...])
            ops_out[0] = ops
            pot_out[0] = pot_row
        else:
            ops = ops_ref[0]
            pot_row = pot_ref[0]
        product = jnp.dot(ops[:, :body_rows], main_rows, preferred_element_type=jnp.float32)
        product = product + jnp.dot(ops[:, body_rows:], tail_rows, preferred_element_type=jnp.float32)
        scale = scales[cell]
        pot = jnp.transpose(jnp.broadcast_to(pot_row, (8, width)))[:, 0:1]
        top = product[:body_rows] * scale + pot[:body_rows] * main_rows.astype(jnp.float32)
        bottom = product[body_rows:] * scale + pot[body_rows:] * tail_rows.astype(jnp.float32)
        local_out[pl.ds(start, body_rows), :] += top
        local_out[pl.ds(tail, quarter), :] += bottom

        @pl.when(cell == pl.num_programs(0) - 1)
        def _():
            for side in range(2):
                def pick(p, carry):
                    n = faces[side * face_half + p]
                    faces_out[side][pl.ds(p, 1), :] = local_out[pl.ds(n, 1), :]
                    return carry

                lax.fori_loop(0, face_half, pick, 0, unroll=8)


def field_step(faces, scales, window_ops, window_pot, vector=None, local_in=None,
               received=None, older=None, alpha=1.0, apply=True, kinetic=None):
    combine = local_in is not None
    has_older = older is not None
    build = kinetic is not None
    node_total, cols = (local_in if combine else vector).shape
    face_half = faces.shape[0] // 2
    cells, width = window_pot.shape[0], window_pot.shape[-1]
    smem = pl.BlockSpec(memory_space=pltpu.SMEM)
    whole = pl.BlockSpec(memory_space=pltpu.VMEM)
    args, specs = [faces], [smem]
    if apply:
        args.append(scales); specs.append(smem)
    if combine:
        args += [local_in, *received]; specs += [whole, whole, whole]
        if has_older:
            args.append(older); specs.append(whole)
    else:
        args.append(vector); specs.append(whole)
    cell_block = pl.BlockSpec((1, width, width), lambda c: (c, 0, 0))
    row_block = pl.BlockSpec((1, 1, width), lambda c: (c, 0, 0))
    if apply:
        args += [window_ops, window_pot]
        specs += [row_block if build else cell_block, row_block]
        if build:
            args.append(kinetic); specs.append(whole)
    out_shape, out_specs = [], []
    if combine:
        out_shape.append(jax.ShapeDtypeStruct((node_total, cols), jnp.bfloat16)); out_specs.append(whole)
    if apply:
        out_shape += [jax.ShapeDtypeStruct((node_total, cols), jnp.float32),
                      jax.ShapeDtypeStruct((face_half, cols), jnp.float32),
                      jax.ShapeDtypeStruct((face_half, cols), jnp.float32)]
        out_specs += [whole, whole, whole]
        if build:
            out_shape += [jax.ShapeDtypeStruct((cells, width, width), jnp.bfloat16),
                          jax.ShapeDtypeStruct((cells, 1, width), jnp.float32)]
            out_specs += [cell_block, row_block]
    scratch = [pltpu.VMEM((node_total, cols), jnp.float32)] if combine else []
    flops = (2 * cells * width * width * cols if apply else 0) + (4 * cells * width ** 3 if build else 0)
    result = pl.pallas_call(
        functools.partial(field_kernel, combine, has_older, apply, build, alpha),
        grid=(cells if apply else 1,),
        in_specs=specs,
        out_specs=out_specs,
        out_shape=out_shape,
        scratch_shapes=scratch,
        compiler_params=pltpu.CompilerParams(
            dimension_semantics=("arbitrary",), vmem_limit_bytes=VMEM_LIMIT),
        cost_estimate=pl.CostEstimate(
            flops=flops, transcendentals=0,
            bytes_accessed=(cells * width * width * 2 if apply else 0) + node_total * cols * 12),
    )(*args)
    return result


def build_operator(slot_row, pot_row, kinetic):
    width = kinetic.shape[0]
    picks = (lax.broadcasted_iota(jnp.int32, (width, width), 0) == slot_row).astype(jnp.bfloat16)
    columns = lax.dot_general(
        kinetic, picks, (((1,), (1,)), ((), ())), preferred_element_type=jnp.float32
    ).astype(jnp.bfloat16)
    ops = jnp.dot(picks, columns, preferred_element_type=jnp.float32).astype(jnp.bfloat16)
    high = pot_row.astype(jnp.bfloat16)
    rest = pot_row - high.astype(jnp.float32)
    middle = rest.astype(jnp.bfloat16)
    low = (rest - middle.astype(jnp.float32)).astype(jnp.bfloat16)
    parts = jnp.concatenate(
        [high, middle, low, jnp.zeros((5, width), jnp.bfloat16)], axis=0
    )
    moved = lax.dot_general(
        parts, picks, (((1,), (1,)), ((), ())), preferred_element_type=jnp.float32
    )
    return ops, moved[0:1] + moved[1:2] + moved[2:3]


def newton(gram_matrix):
    identity = jnp.eye(gram_matrix.shape[0], dtype=jnp.float32)
    frobenius = jnp.sqrt(jnp.sum(gram_matrix * gram_matrix))
    scaled = gram_matrix / frobenius
    inverse_root = identity
    for repeat in range(NS_ITERS):
        factor = 1.5 * identity - 0.5 * jnp.dot(
            inverse_root, scaled, precision=lax.Precision.HIGHEST
        )
        scaled = jnp.dot(scaled, factor, precision=lax.Precision.HIGHEST)
        inverse_root = jnp.dot(factor, inverse_root, precision=lax.Precision.HIGHEST)
    return inverse_root.astype(jnp.bfloat16)


def doubling_sum(value):
    band_size = lax.axis_size("band")
    count = lax.axis_size("dom") * band_size
    bits = list(range(count.bit_length() - 1))
    order = bits[2:3] + bits[0:2] + bits[3:]
    total = value
    for bit in order:
        mask = 1 << bit
        pairs = [(i, i ^ mask) for i in range(count)]
        total = total + lax.ppermute(total, ("dom", "band"), pairs)
    return total


def body(states, cell_kinetic, cell_scale, cell_potential, connectivity, shared_nodes, cell_counts):
    left_face = shared_nodes[0, 0]
    right_face = shared_nodes[0, 1]
    face_width = left_face.shape[0]
    faces = jnp.concatenate([left_face, right_face])
    live_count = cell_counts[0]
    domain = lax.axis_index("dom")
    domains = lax.axis_size("dom")
    node_total = states.shape[1]
    state_cols = states.shape[0]
    has_left = (domain > 0).astype(jnp.float32)
    has_right = (domain < domains - 1).astype(jnp.float32)
    face_counts = jnp.concatenate(
        [jnp.full((face_width,), has_left), jnp.full((face_width,), has_right)]
    )
    node_weight = (
        jnp.ones((node_total,), jnp.float32)
        .at[faces]
        .set(1.0 / (1.0 + face_counts), unique_indices=True)
        .astype(jnp.bfloat16)
    )
    cells, width = connectivity.shape
    starts = jnp.arange(cells, dtype=jnp.int32) * (3 * (width // 4))
    slots = (connectivity - starts[:, None]) % node_total
    alive = (jnp.arange(cells) < live_count).astype(jnp.float32)
    scales = cell_scale * alive
    slot_rows = slots.reshape(cells, 1, width)
    potential_rows = (cell_potential * alive[:, None]).reshape(cells, 1, width)
    up = [(i, i + 1) for i in range(domains - 1)]
    down = [(j, i) for i, j in up]

    def exchange(left_values, right_values):
        from_left = lax.ppermute(right_values, "dom", up)
        from_right = lax.ppermute(left_values, "dom", down)
        return (from_left, from_right)

    first = states.T
    local_sum, *face_values, window_ops, window_pot = field_step(
        faces, scales, slot_rows, potential_rows, vector=first, kinetic=cell_kinetic
    )
    step = functools.partial(field_step, faces, scales, window_ops, window_pot)
    second, local_sum, *face_values = step(local_in=local_sum, received=exchange(*face_values))
    history = [first, second]
    for repeat in range(CHEB - 2):
        following, local_sum, *face_values = step(
            local_in=local_sum, received=exchange(*face_values), older=history[-2], alpha=2.0
        )
        history.append(following)
    (current,) = step(
        local_in=local_sum, received=exchange(*face_values), older=history[-2], alpha=2.0,
        apply=False,
    )
    row_shard = lax.all_to_all(current, "band", split_axis=0, concat_axis=1, tiled=True)
    piece_nodes = row_shard.shape[0]
    weight_rows = lax.dynamic_slice_in_dim(
        node_weight, lax.axis_index("band") * piece_nodes, piece_nodes, 0
    )
    weighted = row_shard * weight_rows[:, None]
    partial_gram = lax.dot_general(
        weighted, row_shard, (((0,), (0,)), ((), ())), preferred_element_type=jnp.float32
    )
    gram_matrix = doubling_sum(partial_gram)
    mixing = newton(gram_matrix)
    rotated = lax.dot_general(
        row_shard, mixing, (((1,), (0,)), ((), ())), preferred_element_type=jnp.float32
    ).astype(jnp.bfloat16)
    back = lax.all_to_all(rotated, "band", split_axis=1, concat_axis=0, tiled=True)
    return back.T


def solution(mesh):
    in_specs = (
        P("band", "dom"),
        P(),
        P("dom"),
        P("dom", None),
        P("dom", None),
        P("dom", None, None),
        P("dom"),
    )
    out_specs = P("band", "dom")
    return jax.shard_map(body, mesh=mesh, in_specs=in_specs, out_specs=out_specs, check_vma=False)
```

```python
import functools

import jax
import jax.numpy as jnp
from jax import lax
from jax.experimental import pallas as pl
from jax.experimental.pallas import tpu as pltpu
from jax.sharding import PartitionSpec as P

CHEB = 4
NS_ITERS = 5


VMEM_LIMIT = 60 * 1024 * 1024


def field_kernel(combine, older, apply, build, alpha, *refs):
    refs = list(refs)
    faces = refs.pop(0)
    if apply:
        scales = refs.pop(0)
    if combine:
        local_in = refs.pop(0)
        received = (refs.pop(0), refs.pop(0))
        if older:
            older_ref = refs.pop(0)
    else:
        vector_in = refs.pop(0)
    if apply:
        ops_ref = refs.pop(0)
        pot_ref = refs.pop(0)
        if build:
            kinetic_ref = refs.pop(0)
    if combine:
        vector_out = refs.pop(0)
    if apply:
        local_out = refs.pop(0)
        faces_out = (refs.pop(0), refs.pop(0))
        if build:
            ops_out = refs.pop(0)
            pot_out = refs.pop(0)
    if combine:
        work = refs.pop(0)
    vector = vector_out if combine else vector_in
    face_half = faces.shape[0] // 2
    node_total = (local_in if combine else vector_in).shape[0]
    cell = pl.program_id(0) if apply else None

    def prologue():
        work[...] = local_in[...] if alpha == 1.0 else alpha * local_in[...]

        for side in range(2):
            def fix(p, carry):
                n = faces[side * face_half + p]
                row = received[side][pl.ds(p, 1), :]
                work[pl.ds(n, 1), :] += row if alpha == 1.0 else alpha * row
                return carry

            lax.fori_loop(0, face_half, fix, 0, unroll=8)
        value = work[...]
        if older:
            value = value - older_ref[...].astype(jnp.float32)
        if apply:
            vector_out[...] = value.astype(vector_out.dtype)
        else:
            work[...] = value
            lanes = 128

            def turn(j, carry):
                rows = pl.ds(pl.multiple_of(j * lanes, lanes), lanes)
                vector_out[:, rows] = jnp.transpose(work[rows, :]).astype(vector_out.dtype)
                return carry

            lax.fori_loop(0, node_total // lanes, turn, 0)

    if combine:
        if apply:
            pl.when(cell == 0)(prologue)
        else:
            prologue()

    if apply:
        width = ops_ref.shape[-1]
        quarter = width // 4
        body_rows = width - quarter

        @pl.when(cell == 0)
        def _():
            local_out[...] = jnp.zeros_like(local_out)

        start = pl.multiple_of(cell * body_rows, quarter)
        tail = pl.multiple_of(lax.rem((cell + 1) * body_rows, node_total), quarter)
        main_rows = vector[pl.ds(start, body_rows), :]
        tail_rows = vector[pl.ds(tail, quarter), :]
        if build:
            ops, pot_row = build_operator(ops_ref[0], pot_ref[0], kinetic_ref[...])
            ops_out[0] = ops
            pot_out[0] = pot_row
        else:
            ops = ops_ref[0]
            pot_row = pot_ref[0]
        product = jnp.dot(ops[:, :body_rows], main_rows, preferred_element_type=jnp.float32)
        product = product + jnp.dot(ops[:, body_rows:], tail_rows, preferred_element_type=jnp.float32)
        scale = scales[cell]
        pot = jnp.transpose(jnp.broadcast_to(pot_row, (8, width)))[:, 0:1]
        top = product[:body_rows] * scale + pot[:body_rows] * main_rows.astype(jnp.float32)
        bottom = product[body_rows:] * scale + pot[body_rows:] * tail_rows.astype(jnp.float32)
        local_out[pl.ds(start, body_rows), :] += top
        local_out[pl.ds(tail, quarter), :] += bottom

        @pl.when(cell == pl.num_programs(0) - 1)
        def _():
            for side in range(2):
                def pick(p, carry):
                    n = faces[side * face_half + p]
                    faces_out[side][pl.ds(p, 1), :] = local_out[pl.ds(n, 1), :]
                    return carry

                lax.fori_loop(0, face_half, pick, 0, unroll=8)


def field_step(faces, scales, window_ops, window_pot, vector=None, local_in=None,
               received=None, older=None, alpha=1.0, apply=True, kinetic=None):
    combine = local_in is not None
    has_older = older is not None
    build = kinetic is not None
    node_total, cols = (local_in if combine else vector).shape
    face_half = faces.shape[0] // 2
    cells, width = window_pot.shape[0], window_pot.shape[-1]
    smem = pl.BlockSpec(memory_space=pltpu.SMEM)
    whole = pl.BlockSpec(memory_space=pltpu.VMEM)
    args, specs = [faces], [smem]
    if apply:
        args.append(scales); specs.append(smem)
    if combine:
        args += [local_in, *received]; specs += [whole, whole, whole]
        if has_older:
            args.append(older); specs.append(whole)
    else:
        args.append(vector); specs.append(whole)
    cell_block = pl.BlockSpec((1, width, width), lambda c: (c, 0, 0))
    row_block = pl.BlockSpec((1, 1, width), lambda c: (c, 0, 0))
    if apply:
        args += [window_ops, window_pot]
        specs += [row_block if build else cell_block, row_block]
        if build:
            args.append(kinetic); specs.append(whole)
    out_shape, out_specs = [], []
    if combine:
        shape = (node_total, cols) if apply else (cols, node_total)
        out_shape.append(jax.ShapeDtypeStruct(shape, jnp.bfloat16)); out_specs.append(whole)
    if apply:
        out_shape += [jax.ShapeDtypeStruct((node_total, cols), jnp.float32),
                      jax.ShapeDtypeStruct((face_half, cols), jnp.float32),
                      jax.ShapeDtypeStruct((face_half, cols), jnp.float32)]
        out_specs += [whole, whole, whole]
        if build:
            out_shape += [jax.ShapeDtypeStruct((cells, width, width), jnp.bfloat16),
                          jax.ShapeDtypeStruct((cells, 1, width), jnp.float32)]
            out_specs += [cell_block, row_block]
    scratch = [pltpu.VMEM((node_total, cols), jnp.float32)] if combine else []
    flops = (2 * cells * width * width * cols if apply else 0) + (4 * cells * width ** 3 if build else 0)
    result = pl.pallas_call(
        functools.partial(field_kernel, combine, has_older, apply, build, alpha),
        grid=(cells if apply else 1,),
        in_specs=specs,
        out_specs=out_specs,
        out_shape=out_shape,
        scratch_shapes=scratch,
        compiler_params=pltpu.CompilerParams(
            dimension_semantics=("arbitrary",), vmem_limit_bytes=VMEM_LIMIT),
        cost_estimate=pl.CostEstimate(
            flops=flops, transcendentals=0,
            bytes_accessed=(cells * width * width * 2 if apply else 0) + node_total * cols * 12),
    )(*args)
    return result


def build_operator(slot_row, pot_row, kinetic):
    width = kinetic.shape[0]
    picks = (lax.broadcasted_iota(jnp.int32, (width, width), 0) == slot_row).astype(jnp.bfloat16)
    columns = lax.dot_general(
        kinetic, picks, (((1,), (1,)), ((), ())), preferred_element_type=jnp.float32
    ).astype(jnp.bfloat16)
    ops = jnp.dot(picks, columns, preferred_element_type=jnp.float32).astype(jnp.bfloat16)
    high = pot_row.astype(jnp.bfloat16)
    rest = pot_row - high.astype(jnp.float32)
    middle = rest.astype(jnp.bfloat16)
    low = (rest - middle.astype(jnp.float32)).astype(jnp.bfloat16)
    parts = jnp.concatenate(
        [high, middle, low, jnp.zeros((5, width), jnp.bfloat16)], axis=0
    )
    moved = lax.dot_general(
        parts, picks, (((1,), (1,)), ((), ())), preferred_element_type=jnp.float32
    )
    return ops, moved[0:1] + moved[1:2] + moved[2:3]


def newton(gram_matrix):
    identity = jnp.eye(gram_matrix.shape[0], dtype=jnp.float32)
    frobenius = jnp.sqrt(jnp.sum(gram_matrix * gram_matrix))
    scaled = gram_matrix / frobenius
    inverse_root = identity
    for repeat in range(NS_ITERS):
        factor = 1.5 * identity - 0.5 * jnp.dot(
            inverse_root, scaled, precision=lax.Precision.HIGHEST
        )
        scaled = jnp.dot(scaled, factor, precision=lax.Precision.HIGHEST)
        inverse_root = jnp.dot(factor, inverse_root, precision=lax.Precision.HIGHEST)
    return inverse_root.astype(jnp.bfloat16)


def doubling_sum(value):
    band_size = lax.axis_size("band")
    count = lax.axis_size("dom") * band_size
    bits = list(range(count.bit_length() - 1))
    order = bits[2:3] + bits[0:2] + bits[3:]
    total = value
    for bit in order:
        mask = 1 << bit
        pairs = [(i, i ^ mask) for i in range(count)]
        total = total + lax.ppermute(total, ("dom", "band"), pairs)
    return total


def body(states, cell_kinetic, cell_scale, cell_potential, connectivity, shared_nodes, cell_counts):
    left_face = shared_nodes[0, 0]
    right_face = shared_nodes[0, 1]
    face_width = left_face.shape[0]
    faces = jnp.concatenate([left_face, right_face])
    live_count = cell_counts[0]
    domain = lax.axis_index("dom")
    domains = lax.axis_size("dom")
    node_total = states.shape[1]
    state_cols = states.shape[0]
    has_left = (domain > 0).astype(jnp.float32)
    has_right = (domain < domains - 1).astype(jnp.float32)
    face_counts = jnp.concatenate(
        [jnp.full((face_width,), has_left), jnp.full((face_width,), has_right)]
    )
    node_weight = (
        jnp.ones((node_total,), jnp.float32)
        .at[faces]
        .set(1.0 / (1.0 + face_counts), unique_indices=True)
        .astype(jnp.bfloat16)
    )
    cells, width = connectivity.shape
    starts = jnp.arange(cells, dtype=jnp.int32) * (3 * (width // 4))
    slots = (connectivity - starts[:, None]) % node_total
    alive = (jnp.arange(cells) < live_count).astype(jnp.float32)
    scales = cell_scale * alive
    slot_rows = slots.reshape(cells, 1, width)
    potential_rows = (cell_potential * alive[:, None]).reshape(cells, 1, width)
    up = [(i, i + 1) for i in range(domains - 1)]
    down = [(j, i) for i, j in up]

    def exchange(left_values, right_values):
        from_left = lax.ppermute(right_values, "dom", up)
        from_right = lax.ppermute(left_values, "dom", down)
        return (from_left, from_right)

    first = states.T
    local_sum, *face_values, window_ops, window_pot = field_step(
        faces, scales, slot_rows, potential_rows, vector=first, kinetic=cell_kinetic
    )
    step = functools.partial(field_step, faces, scales, window_ops, window_pot)
    second, local_sum, *face_values = step(local_in=local_sum, received=exchange(*face_values))
    history = [first, second]
    for repeat in range(CHEB - 2):
        following, local_sum, *face_values = step(
            local_in=local_sum, received=exchange(*face_values), older=history[-2], alpha=2.0
        )
        history.append(following)
    (current,) = step(
        local_in=local_sum, received=exchange(*face_values), older=history[-2], alpha=2.0,
        apply=False,
    )
    row_shard = lax.all_to_all(current, "band", split_axis=1, concat_axis=0, tiled=True)
    piece_nodes = row_shard.shape[1]
    weight_rows = lax.dynamic_slice_in_dim(
        node_weight, lax.axis_index("band") * piece_nodes, piece_nodes, 0
    )
    weighted = row_shard * weight_rows[None]
    partial_gram = lax.dot_general(
        weighted, row_shard, (((1,), (1,)), ((), ())), preferred_element_type=jnp.float32
    )
    gram_matrix = doubling_sum(partial_gram)
    mixing = newton(gram_matrix)
    rotated = lax.dot_general(
        mixing, row_shard, (((0,), (0,)), ((), ())), preferred_element_type=jnp.float32
    ).astype(jnp.bfloat16)
    return lax.all_to_all(rotated, "band", split_axis=0, concat_axis=1, tiled=True)


def solution(mesh):
    in_specs = (
        P("band", "dom"),
        P(),
        P("dom"),
        P("dom", None),
        P("dom", None),
        P("dom", None, None),
        P("dom"),
    )
    out_specs = P("band", "dom")
    return jax.shard_map(body, mesh=mesh, in_specs=in_specs, out_specs=out_specs, check_vma=False)
```

```python
import functools

import jax
import jax.numpy as jnp
from jax import lax
from jax.experimental import pallas as pl
from jax.experimental.pallas import tpu as pltpu
from jax.sharding import PartitionSpec as P

CHEB = 4
NS_ITERS = 5


VMEM_LIMIT = 60 * 1024 * 1024
GROUP = 2


def field_kernel(combine, older, apply, build, alpha, *refs):
    refs = list(refs)
    faces = refs.pop(0)
    if apply:
        scales = refs.pop(0)
    if combine:
        local_in = refs.pop(0)
        received = (refs.pop(0), refs.pop(0))
        if older:
            older_ref = refs.pop(0)
    else:
        vector_in = refs.pop(0)
    if apply:
        ops_ref = refs.pop(0)
        pot_ref = refs.pop(0)
        if build:
            kinetic_ref = refs.pop(0)
    if combine:
        vector_out = refs.pop(0)
    if apply:
        local_out = refs.pop(0)
        faces_out = (refs.pop(0), refs.pop(0))
        if build:
            ops_out = refs.pop(0)
            pot_out = refs.pop(0)
    if combine:
        work = refs.pop(0)
    vector = vector_out if combine else vector_in
    face_half = faces.shape[0] // 2
    node_total = vector.shape[0]
    cell = pl.program_id(0) if apply else None

    def prologue():
        work[...] = local_in[...] if alpha == 1.0 else alpha * local_in[...]

        for side in range(2):
            def fix(p, carry):
                n = faces[side * face_half + p]
                row = received[side][pl.ds(p, 1), :]
                work[pl.ds(n, 1), :] += row if alpha == 1.0 else alpha * row
                return carry

            lax.fori_loop(0, face_half, fix, 0, unroll=8)
        value = work[...]
        if older:
            value = value - older_ref[...].astype(jnp.float32)
        vector_out[...] = value.astype(vector_out.dtype)

    if combine:
        if apply:
            pl.when(cell == 0)(prologue)
        else:
            prologue()

    if apply:
        width = ops_ref.shape[-1]
        quarter = width // 4
        body_rows = width - quarter

        @pl.when(cell == 0)
        def _():
            local_out[...] = jnp.zeros_like(local_out)

        for k in range(GROUP):
            index = cell * GROUP + k
            start = pl.multiple_of(index * body_rows, quarter)
            tail = pl.multiple_of(lax.rem((index + 1) * body_rows, node_total), quarter)
            main_rows = vector[pl.ds(start, body_rows), :]
            tail_rows = vector[pl.ds(tail, quarter), :]
            if build:
                ops, pot_row = build_operator(ops_ref[k], pot_ref[k], kinetic_ref[...])
                ops_out[k] = ops
                pot_out[k] = pot_row
            else:
                ops = ops_ref[k]
                pot_row = pot_ref[k]
            product = jnp.dot(ops[:, :body_rows], main_rows, preferred_element_type=jnp.float32)
            product = product + jnp.dot(
                ops[:, body_rows:], tail_rows, preferred_element_type=jnp.float32
            )
            scale = scales[index]
            pot = jnp.transpose(jnp.broadcast_to(pot_row, (8, width)))[:, 0:1]
            top = product[:body_rows] * scale + pot[:body_rows] * main_rows.astype(jnp.float32)
            bottom = product[body_rows:] * scale + pot[body_rows:] * tail_rows.astype(jnp.float32)
            local_out[pl.ds(start, body_rows), :] += top
            local_out[pl.ds(tail, quarter), :] += bottom

        @pl.when(cell == pl.num_programs(0) - 1)
        def _():
            for side in range(2):
                def pick(p, carry):
                    n = faces[side * face_half + p]
                    faces_out[side][pl.ds(p, 1), :] = local_out[pl.ds(n, 1), :]
                    return carry

                lax.fori_loop(0, face_half, pick, 0, unroll=8)


def field_step(faces, scales, window_ops, window_pot, vector=None, local_in=None,
               received=None, older=None, alpha=1.0, apply=True, kinetic=None):
    combine = local_in is not None
    has_older = older is not None
    build = kinetic is not None
    node_total, cols = (local_in if combine else vector).shape
    face_half = faces.shape[0] // 2
    cells, width = window_pot.shape[0], window_pot.shape[-1]
    smem = pl.BlockSpec(memory_space=pltpu.SMEM)
    whole = pl.BlockSpec(memory_space=pltpu.VMEM)
    args, specs = [faces], [smem]
    if apply:
        args.append(scales); specs.append(smem)
    if combine:
        args += [local_in, *received]; specs += [whole, whole, whole]
        if has_older:
            args.append(older); specs.append(whole)
    else:
        args.append(vector); specs.append(whole)
    cell_block = pl.BlockSpec((GROUP, width, width), lambda c: (c, 0, 0))
    row_block = pl.BlockSpec((GROUP, 1, width), lambda c: (c, 0, 0))
    if apply:
        args += [window_ops, window_pot]
        specs += [row_block if build else cell_block, row_block]
        if build:
            args.append(kinetic); specs.append(whole)
    out_shape, out_specs = [], []
    if combine:
        out_shape.append(jax.ShapeDtypeStruct((node_total, cols), jnp.bfloat16)); out_specs.append(whole)
    if apply:
        out_shape += [jax.ShapeDtypeStruct((node_total, cols), jnp.float32),
                      jax.ShapeDtypeStruct((face_half, cols), jnp.float32),
                      jax.ShapeDtypeStruct((face_half, cols), jnp.float32)]
        out_specs += [whole, whole, whole]
        if build:
            out_shape += [jax.ShapeDtypeStruct((cells, width, width), jnp.bfloat16),
                          jax.ShapeDtypeStruct((cells, 1, width), jnp.float32)]
            out_specs += [cell_block, row_block]
    scratch = [pltpu.VMEM((node_total, cols), jnp.float32)] if combine else []
    flops = (2 * cells * width * width * cols if apply else 0) + (4 * cells * width ** 3 if build else 0)
    result = pl.pallas_call(
        functools.partial(field_kernel, combine, has_older, apply, build, alpha),
        grid=(cells // GROUP if apply else 1,),
        in_specs=specs,
        out_specs=out_specs,
        out_shape=out_shape,
        scratch_shapes=scratch,
        compiler_params=pltpu.CompilerParams(
            dimension_semantics=("arbitrary",), vmem_limit_bytes=VMEM_LIMIT),
        cost_estimate=pl.CostEstimate(
            flops=flops, transcendentals=0,
            bytes_accessed=(cells * width * width * 2 if apply else 0) + node_total * cols * 12),
    )(*args)
    return result


def build_operator(slot_row, pot_row, kinetic):
    width = kinetic.shape[0]
    picks = (lax.broadcasted_iota(jnp.int32, (width, width), 0) == slot_row).astype(jnp.bfloat16)
    columns = lax.dot_general(
        kinetic, picks, (((1,), (1,)), ((), ())), preferred_element_type=jnp.float32
    ).astype(jnp.bfloat16)
    ops = jnp.dot(picks, columns, preferred_element_type=jnp.float32).astype(jnp.bfloat16)
    high = pot_row.astype(jnp.bfloat16)
    rest = pot_row - high.astype(jnp.float32)
    middle = rest.astype(jnp.bfloat16)
    low = (rest - middle.astype(jnp.float32)).astype(jnp.bfloat16)
    parts = jnp.concatenate(
        [high, middle, low, jnp.zeros((5, width), jnp.bfloat16)], axis=0
    )
    moved = lax.dot_general(
        parts, picks, (((1,), (1,)), ((), ())), preferred_element_type=jnp.float32
    )
    return ops, moved[0:1] + moved[1:2] + moved[2:3]


def newton(gram_matrix):
    identity = jnp.eye(gram_matrix.shape[0], dtype=jnp.float32)
    frobenius = jnp.sqrt(jnp.sum(gram_matrix * gram_matrix))
    scaled = gram_matrix / frobenius
    inverse_root = identity
    for repeat in range(NS_ITERS):
        factor = 1.5 * identity - 0.5 * jnp.dot(
            inverse_root, scaled, precision=lax.Precision.HIGHEST
        )
        scaled = jnp.dot(scaled, factor, precision=lax.Precision.HIGHEST)
        inverse_root = jnp.dot(factor, inverse_root, precision=lax.Precision.HIGHEST)
    return inverse_root.astype(jnp.bfloat16)


def doubling_sum(value):
    band_size = lax.axis_size("band")
    count = lax.axis_size("dom") * band_size
    bits = list(range(count.bit_length() - 1))
    order = bits[2:3] + bits[0:2] + bits[3:]
    total = value
    for bit in order:
        mask = 1 << bit
        pairs = [(i, i ^ mask) for i in range(count)]
        total = total + lax.ppermute(total, ("dom", "band"), pairs)
    return total


def body(states, cell_kinetic, cell_scale, cell_potential, connectivity, shared_nodes, cell_counts):
    left_face = shared_nodes[0, 0]
    right_face = shared_nodes[0, 1]
    face_width = left_face.shape[0]
    faces = jnp.concatenate([left_face, right_face])
    live_count = cell_counts[0]
    domain = lax.axis_index("dom")
    domains = lax.axis_size("dom")
    node_total = states.shape[1]
    state_cols = states.shape[0]
    has_left = (domain > 0).astype(jnp.float32)
    has_right = (domain < domains - 1).astype(jnp.float32)
    face_counts = jnp.concatenate(
        [jnp.full((face_width,), has_left), jnp.full((face_width,), has_right)]
    )
    node_weight = (
        jnp.ones((node_total,), jnp.float32)
        .at[faces]
        .set(1.0 / (1.0 + face_counts), unique_indices=True)
        .astype(jnp.bfloat16)
    )
    cells, width = connectivity.shape
    starts = jnp.arange(cells, dtype=jnp.int32) * (3 * (width // 4))
    slots = (connectivity - starts[:, None]) % node_total
    alive = (jnp.arange(cells) < live_count).astype(jnp.float32)
    scales = cell_scale * alive
    slot_rows = slots.reshape(cells, 1, width)
    potential_rows = (cell_potential * alive[:, None]).reshape(cells, 1, width)
    up = [(i, i + 1) for i in range(domains - 1)]
    down = [(j, i) for i, j in up]

    def exchange(left_values, right_values):
        from_left = lax.ppermute(right_values, "dom", up)
        from_right = lax.ppermute(left_values, "dom", down)
        return (from_left, from_right)

    first = states.T
    local_sum, *face_values, window_ops, window_pot = field_step(
        faces, scales, slot_rows, potential_rows, vector=first, kinetic=cell_kinetic
    )
    step = functools.partial(field_step, faces, scales, window_ops, window_pot)
    second, local_sum, *face_values = step(local_in=local_sum, received=exchange(*face_values))
    history = [first, second]
    for repeat in range(CHEB - 2):
        following, local_sum, *face_values = step(
            local_in=local_sum, received=exchange(*face_values), older=history[-2], alpha=2.0
        )
        history.append(following)
    (current,) = step(
        local_in=local_sum, received=exchange(*face_values), older=history[-2], alpha=2.0,
        apply=False,
    )
    row_shard = lax.all_to_all(current, "band", split_axis=0, concat_axis=1, tiled=True)
    piece_nodes = row_shard.shape[0]
    weight_rows = lax.dynamic_slice_in_dim(
        node_weight, lax.axis_index("band") * piece_nodes, piece_nodes, 0
    )
    weighted = row_shard * weight_rows[:, None]
    partial_gram = lax.dot_general(
        weighted, row_shard, (((0,), (0,)), ((), ())), preferred_element_type=jnp.float32
    )
    gram_matrix = doubling_sum(partial_gram)
    mixing = newton(gram_matrix)
    rotated = lax.dot_general(
        row_shard, mixing, (((1,), (0,)), ((), ())), preferred_element_type=jnp.float32
    ).astype(jnp.bfloat16)
    back = lax.all_to_all(rotated, "band", split_axis=1, concat_axis=0, tiled=True)
    return back.T


def solution(mesh):
    in_specs = (
        P("band", "dom"),
        P(),
        P("dom"),
        P("dom", None),
        P("dom", None),
        P("dom", None, None),
        P("dom"),
    )
    out_specs = P("band", "dom")
    return jax.shard_map(body, mesh=mesh, in_specs=in_specs, out_specs=out_specs, check_vma=False)
```

```python
import functools

import jax
import jax.numpy as jnp
from jax import lax
from jax.experimental import pallas as pl
from jax.experimental.pallas import tpu as pltpu
from jax.sharding import PartitionSpec as P

CHEB = 4
NS_ITERS = 5


VMEM_LIMIT = 60 * 1024 * 1024
GROUP = 4


def field_kernel(combine, older, apply, build, alpha, *refs):
    refs = list(refs)
    faces = refs.pop(0)
    if apply:
        scales = refs.pop(0)
    if combine:
        local_in = refs.pop(0)
        received = (refs.pop(0), refs.pop(0))
        if older:
            older_ref = refs.pop(0)
    else:
        vector_in = refs.pop(0)
    if apply:
        ops_ref = refs.pop(0)
        pot_ref = refs.pop(0)
        if build:
            kinetic_ref = refs.pop(0)
    if combine:
        vector_out = refs.pop(0)
    if apply:
        local_out = refs.pop(0)
        faces_out = (refs.pop(0), refs.pop(0))
        if build:
            ops_out = refs.pop(0)
            pot_out = refs.pop(0)
    if combine:
        work = refs.pop(0)
    vector = vector_out if combine else vector_in
    face_half = faces.shape[0] // 2
    node_total = vector.shape[0]
    cell = pl.program_id(0) if apply else None

    def prologue():
        work[...] = local_in[...] if alpha == 1.0 else alpha * local_in[...]

        for side in range(2):
            def fix(p, carry):
                n = faces[side * face_half + p]
                row = received[side][pl.ds(p, 1), :]
                work[pl.ds(n, 1), :] += row if alpha == 1.0 else alpha * row
                return carry

            lax.fori_loop(0, face_half, fix, 0, unroll=8)
        value = work[...]
        if older:
            value = value - older_ref[...].astype(jnp.float32)
        vector_out[...] = value.astype(vector_out.dtype)

    if combine:
        if apply:
            pl.when(cell == 0)(prologue)
        else:
            prologue()

    if apply:
        width = ops_ref.shape[-1]
        quarter = width // 4
        body_rows = width - quarter

        @pl.when(cell == 0)
        def _():
            local_out[...] = jnp.zeros_like(local_out)

        for k in range(GROUP):
            index = cell * GROUP + k
            start = pl.multiple_of(index * body_rows, quarter)
            tail = pl.multiple_of(lax.rem((index + 1) * body_rows, node_total), quarter)
            main_rows = vector[pl.ds(start, body_rows), :]
            tail_rows = vector[pl.ds(tail, quarter), :]
            if build:
                ops, pot_row = build_operator(ops_ref[k], pot_ref[k], kinetic_ref[...])
                ops_out[k] = ops
                pot_out[k] = pot_row
            else:
                ops = ops_ref[k]
                pot_row = pot_ref[k]
            product = jnp.dot(ops[:, :body_rows], main_rows, preferred_element_type=jnp.float32)
            product = product + jnp.dot(
                ops[:, body_rows:], tail_rows, preferred_element_type=jnp.float32
            )
            scale = scales[index]
            pot = jnp.transpose(jnp.broadcast_to(pot_row, (8, width)))[:, 0:1]
            top = product[:body_rows] * scale + pot[:body_rows] * main_rows.astype(jnp.float32)
            bottom = product[body_rows:] * scale + pot[body_rows:] * tail_rows.astype(jnp.float32)
            local_out[pl.ds(start, body_rows), :] += top
            local_out[pl.ds(tail, quarter), :] += bottom

        @pl.when(cell == pl.num_programs(0) - 1)
        def _():
            for side in range(2):
                def pick(p, carry):
                    n = faces[side * face_half + p]
                    faces_out[side][pl.ds(p, 1), :] = local_out[pl.ds(n, 1), :]
                    return carry

                lax.fori_loop(0, face_half, pick, 0, unroll=8)


def field_step(faces, scales, window_ops, window_pot, vector=None, local_in=None,
               received=None, older=None, alpha=1.0, apply=True, kinetic=None):
    combine = local_in is not None
    has_older = older is not None
    build = kinetic is not None
    node_total, cols = (local_in if combine else vector).shape
    face_half = faces.shape[0] // 2
    cells, width = window_pot.shape[0], window_pot.shape[-1]
    smem = pl.BlockSpec(memory_space=pltpu.SMEM)
    whole = pl.BlockSpec(memory_space=pltpu.VMEM)
    args, specs = [faces], [smem]
    if apply:
        args.append(scales); specs.append(smem)
    if combine:
        args += [local_in, *received]; specs += [whole, whole, whole]
        if has_older:
            args.append(older); specs.append(whole)
    else:
        args.append(vector); specs.append(whole)
    cell_block = pl.BlockSpec((GROUP, width, width), lambda c: (c, 0, 0))
    row_block = pl.BlockSpec((GROUP, 1, width), lambda c: (c, 0, 0))
    if apply:
        args += [window_ops, window_pot]
        specs += [row_block if build else cell_block, row_block]
        if build:
            args.append(kinetic); specs.append(whole)
    out_shape, out_specs = [], []
    if combine:
        out_shape.append(jax.ShapeDtypeStruct((node_total, cols), jnp.bfloat16)); out_specs.append(whole)
    if apply:
        out_shape += [jax.ShapeDtypeStruct((node_total, cols), jnp.float32),
                      jax.ShapeDtypeStruct((face_half, cols), jnp.float32),
                      jax.ShapeDtypeStruct((face_half, cols), jnp.float32)]
        out_specs += [whole, whole, whole]
        if build:
            out_shape += [jax.ShapeDtypeStruct((cells, width, width), jnp.bfloat16),
                          jax.ShapeDtypeStruct((cells, 1, width), jnp.float32)]
            out_specs += [cell_block, row_block]
    scratch = [pltpu.VMEM((node_total, cols), jnp.float32)] if combine else []
    flops = (2 * cells * width * width * cols if apply else 0) + (4 * cells * width ** 3 if build else 0)
    result = pl.pallas_call(
        functools.partial(field_kernel, combine, has_older, apply, build, alpha),
        grid=(cells // GROUP if apply else 1,),
        in_specs=specs,
        out_specs=out_specs,
        out_shape=out_shape,
        scratch_shapes=scratch,
        compiler_params=pltpu.CompilerParams(
            dimension_semantics=("arbitrary",), vmem_limit_bytes=VMEM_LIMIT),
        cost_estimate=pl.CostEstimate(
            flops=flops, transcendentals=0,
            bytes_accessed=(cells * width * width * 2 if apply else 0) + node_total * cols * 12),
    )(*args)
    return result


def build_operator(slot_row, pot_row, kinetic):
    width = kinetic.shape[0]
    picks = (lax.broadcasted_iota(jnp.int32, (width, width), 0) == slot_row).astype(jnp.bfloat16)
    columns = lax.dot_general(
        kinetic, picks, (((1,), (1,)), ((), ())), preferred_element_type=jnp.float32
    ).astype(jnp.bfloat16)
    ops = jnp.dot(picks, columns, preferred_element_type=jnp.float32).astype(jnp.bfloat16)
    high = pot_row.astype(jnp.bfloat16)
    rest = pot_row - high.astype(jnp.float32)
    middle = rest.astype(jnp.bfloat16)
    low = (rest - middle.astype(jnp.float32)).astype(jnp.bfloat16)
    parts = jnp.concatenate(
        [high, middle, low, jnp.zeros((5, width), jnp.bfloat16)], axis=0
    )
    moved = lax.dot_general(
        parts, picks, (((1,), (1,)), ((), ())), preferred_element_type=jnp.float32
    )
    return ops, moved[0:1] + moved[1:2] + moved[2:3]


def newton(gram_matrix):
    identity = jnp.eye(gram_matrix.shape[0], dtype=jnp.float32)
    frobenius = jnp.sqrt(jnp.sum(gram_matrix * gram_matrix))
    scaled = gram_matrix / frobenius
    inverse_root = identity
    for repeat in range(NS_ITERS):
        factor = 1.5 * identity - 0.5 * jnp.dot(
            inverse_root, scaled, precision=lax.Precision.HIGHEST
        )
        scaled = jnp.dot(scaled, factor, precision=lax.Precision.HIGHEST)
        inverse_root = jnp.dot(factor, inverse_root, precision=lax.Precision.HIGHEST)
    return inverse_root.astype(jnp.bfloat16)


def doubling_sum(value):
    band_size = lax.axis_size("band")
    count = lax.axis_size("dom") * band_size
    bits = list(range(count.bit_length() - 1))
    order = bits[2:3] + bits[0:2] + bits[3:]
    total = value
    for bit in order:
        mask = 1 << bit
        pairs = [(i, i ^ mask) for i in range(count)]
        total = total + lax.ppermute(total, ("dom", "band"), pairs)
    return total


def body(states, cell_kinetic, cell_scale, cell_potential, connectivity, shared_nodes, cell_counts):
    left_face = shared_nodes[0, 0]
    right_face = shared_nodes[0, 1]
    face_width = left_face.shape[0]
    faces = jnp.concatenate([left_face, right_face])
    live_count = cell_counts[0]
    domain = lax.axis_index("dom")
    domains = lax.axis_size("dom")
    node_total = states.shape[1]
    state_cols = states.shape[0]
    has_left = (domain > 0).astype(jnp.float32)
    has_right = (domain < domains - 1).astype(jnp.float32)
    face_counts = jnp.concatenate(
        [jnp.full((face_width,), has_left), jnp.full((face_width,), has_right)]
    )
    node_weight = (
        jnp.ones((node_total,), jnp.float32)
        .at[faces]
        .set(1.0 / (1.0 + face_counts), unique_indices=True)
        .astype(jnp.bfloat16)
    )
    cells, width = connectivity.shape
    starts = jnp.arange(cells, dtype=jnp.int32) * (3 * (width // 4))
    slots = (connectivity - starts[:, None]) % node_total
    alive = (jnp.arange(cells) < live_count).astype(jnp.float32)
    scales = cell_scale * alive
    slot_rows = slots.reshape(cells, 1, width)
    potential_rows = (cell_potential * alive[:, None]).reshape(cells, 1, width)
    up = [(i, i + 1) for i in range(domains - 1)]
    down = [(j, i) for i, j in up]

    def exchange(left_values, right_values):
        from_left = lax.ppermute(right_values, "dom", up)
        from_right = lax.ppermute(left_values, "dom", down)
        return (from_left, from_right)

    first = states.T
    local_sum, *face_values, window_ops, window_pot = field_step(
        faces, scales, slot_rows, potential_rows, vector=first, kinetic=cell_kinetic
    )
    step = functools.partial(field_step, faces, scales, window_ops, window_pot)
    second, local_sum, *face_values = step(local_in=local_sum, received=exchange(*face_values))
    history = [first, second]
    for repeat in range(CHEB - 2):
        following, local_sum, *face_values = step(
            local_in=local_sum, received=exchange(*face_values), older=history[-2], alpha=2.0
        )
        history.append(following)
    (current,) = step(
        local_in=local_sum, received=exchange(*face_values), older=history[-2], alpha=2.0,
        apply=False,
    )
    row_shard = lax.all_to_all(current, "band", split_axis=0, concat_axis=1, tiled=True)
    piece_nodes = row_shard.shape[0]
    weight_rows = lax.dynamic_slice_in_dim(
        node_weight, lax.axis_index("band") * piece_nodes, piece_nodes, 0
    )
    weighted = row_shard * weight_rows[:, None]
    partial_gram = lax.dot_general(
        weighted, row_shard, (((0,), (0,)), ((), ())), preferred_element_type=jnp.float32
    )
    gram_matrix = doubling_sum(partial_gram)
    mixing = newton(gram_matrix)
    rotated = lax.dot_general(
        row_shard, mixing, (((1,), (0,)), ((), ())), preferred_element_type=jnp.float32
    ).astype(jnp.bfloat16)
    back = lax.all_to_all(rotated, "band", split_axis=1, concat_axis=0, tiled=True)
    return back.T


def solution(mesh):
    in_specs = (
        P("band", "dom"),
        P(),
        P("dom"),
        P("dom", None),
        P("dom", None),
        P("dom", None, None),
        P("dom"),
    )
    out_specs = P("band", "dom")
    return jax.shard_map(body, mesh=mesh, in_specs=in_specs, out_specs=out_specs, check_vma=False)
```

```python
import functools

import jax
import jax.numpy as jnp
from jax import lax
from jax.experimental import pallas as pl
from jax.experimental.pallas import tpu as pltpu
from jax.sharding import PartitionSpec as P

CHEB = 4
NS_ITERS = 5


VMEM_LIMIT = 60 * 1024 * 1024
GROUP = 8


def field_kernel(combine, older, apply, build, alpha, *refs):
    refs = list(refs)
    faces = refs.pop(0)
    if apply:
        scales = refs.pop(0)
    if combine:
        local_in = refs.pop(0)
        received = (refs.pop(0), refs.pop(0))
        if older:
            older_ref = refs.pop(0)
    else:
        vector_in = refs.pop(0)
    if apply:
        ops_ref = refs.pop(0)
        pot_ref = refs.pop(0)
        if build:
            kinetic_ref = refs.pop(0)
    if combine:
        vector_out = refs.pop(0)
    if apply:
        local_out = refs.pop(0)
        faces_out = (refs.pop(0), refs.pop(0))
        if build:
            ops_out = refs.pop(0)
            pot_out = refs.pop(0)
    if combine:
        work = refs.pop(0)
    vector = vector_out if combine else vector_in
    face_half = faces.shape[0] // 2
    node_total = vector.shape[0]
    cell = pl.program_id(0) if apply else None

    def prologue():
        work[...] = local_in[...] if alpha == 1.0 else alpha * local_in[...]

        for side in range(2):
            def fix(p, carry):
                n = faces[side * face_half + p]
                row = received[side][pl.ds(p, 1), :]
                work[pl.ds(n, 1), :] += row if alpha == 1.0 else alpha * row
                return carry

            lax.fori_loop(0, face_half, fix, 0, unroll=8)
        value = work[...]
        if older:
            value = value - older_ref[...].astype(jnp.float32)
        vector_out[...] = value.astype(vector_out.dtype)

    if combine:
        if apply:
            pl.when(cell == 0)(prologue)
        else:
            prologue()

    if apply:
        width = ops_ref.shape[-1]
        quarter = width // 4
        body_rows = width - quarter

        @pl.when(cell == 0)
        def _():
            local_out[...] = jnp.zeros_like(local_out)

        for k in range(GROUP):
            index = cell * GROUP + k
            start = pl.multiple_of(index * body_rows, quarter)
            tail = pl.multiple_of(lax.rem((index + 1) * body_rows, node_total), quarter)
            main_rows = vector[pl.ds(start, body_rows), :]
            tail_rows = vector[pl.ds(tail, quarter), :]
            if build:
                ops, pot_row = build_operator(ops_ref[k], pot_ref[k], kinetic_ref[...])
                ops_out[k] = ops
                pot_out[k] = pot_row
            else:
                ops = ops_ref[k]
                pot_row = pot_ref[k]
            product = jnp.dot(ops[:, :body_rows], main_rows, preferred_element_type=jnp.float32)
            product = product + jnp.dot(
                ops[:, body_rows:], tail_rows, preferred_element_type=jnp.float32
            )
            scale = scales[index]
            pot = jnp.transpose(jnp.broadcast_to(pot_row, (8, width)))[:, 0:1]
            top = product[:body_rows] * scale + pot[:body_rows] * main_rows.astype(jnp.float32)
            bottom = product[body_rows:] * scale + pot[body_rows:] * tail_rows.astype(jnp.float32)
            local_out[pl.ds(start, body_rows), :] += top
            local_out[pl.ds(tail, quarter), :] += bottom

        @pl.when(cell == pl.num_programs(0) - 1)
        def _():
            for side in range(2):
                def pick(p, carry):
                    n = faces[side * face_half + p]
                    faces_out[side][pl.ds(p, 1), :] = local_out[pl.ds(n, 1), :]
                    return carry

                lax.fori_loop(0, face_half, pick, 0, unroll=8)


def field_step(faces, scales, window_ops, window_pot, vector=None, local_in=None,
               received=None, older=None, alpha=1.0, apply=True, kinetic=None):
    combine = local_in is not None
    has_older = older is not None
    build = kinetic is not None
    node_total, cols = (local_in if combine else vector).shape
    face_half = faces.shape[0] // 2
    cells, width = window_pot.shape[0], window_pot.shape[-1]
    smem = pl.BlockSpec(memory_space=pltpu.SMEM)
    whole = pl.BlockSpec(memory_space=pltpu.VMEM)
    args, specs = [faces], [smem]
    if apply:
        args.append(scales); specs.append(smem)
    if combine:
        args += [local_in, *received]; specs += [whole, whole, whole]
        if has_older:
            args.append(older); specs.append(whole)
    else:
        args.append(vector); specs.append(whole)
    cell_block = pl.BlockSpec((GROUP, width, width), lambda c: (c, 0, 0))
    row_block = pl.BlockSpec((GROUP, 1, width), lambda c: (c, 0, 0))
    if apply:
        args += [window_ops, window_pot]
        specs += [row_block if build else cell_block, row_block]
        if build:
            args.append(kinetic); specs.append(whole)
    out_shape, out_specs = [], []
    if combine:
        out_shape.append(jax.ShapeDtypeStruct((node_total, cols), jnp.bfloat16)); out_specs.append(whole)
    if apply:
        out_shape += [jax.ShapeDtypeStruct((node_total, cols), jnp.float32),
                      jax.ShapeDtypeStruct((face_half, cols), jnp.float32),
                      jax.ShapeDtypeStruct((face_half, cols), jnp.float32)]
        out_specs += [whole, whole, whole]
        if build:
            out_shape += [jax.ShapeDtypeStruct((cells, width, width), jnp.bfloat16),
                          jax.ShapeDtypeStruct((cells, 1, width), jnp.float32)]
            out_specs += [cell_block, row_block]
    scratch = [pltpu.VMEM((node_total, cols), jnp.float32)] if combine else []
    flops = (2 * cells * width * width * cols if apply else 0) + (4 * cells * width ** 3 if build else 0)
    result = pl.pallas_call(
        functools.partial(field_kernel, combine, has_older, apply, build, alpha),
        grid=(cells // GROUP if apply else 1,),
        in_specs=specs,
        out_specs=out_specs,
        out_shape=out_shape,
        scratch_shapes=scratch,
        compiler_params=pltpu.CompilerParams(
            dimension_semantics=("arbitrary",), vmem_limit_bytes=VMEM_LIMIT),
        cost_estimate=pl.CostEstimate(
            flops=flops, transcendentals=0,
            bytes_accessed=(cells * width * width * 2 if apply else 0) + node_total * cols * 12),
    )(*args)
    return result


def build_operator(slot_row, pot_row, kinetic):
    width = kinetic.shape[0]
    picks = (lax.broadcasted_iota(jnp.int32, (width, width), 0) == slot_row).astype(jnp.bfloat16)
    columns = lax.dot_general(
        kinetic, picks, (((1,), (1,)), ((), ())), preferred_element_type=jnp.float32
    ).astype(jnp.bfloat16)
    ops = jnp.dot(picks, columns, preferred_element_type=jnp.float32).astype(jnp.bfloat16)
    high = pot_row.astype(jnp.bfloat16)
    rest = pot_row - high.astype(jnp.float32)
    middle = rest.astype(jnp.bfloat16)
    low = (rest - middle.astype(jnp.float32)).astype(jnp.bfloat16)
    parts = jnp.concatenate(
        [high, middle, low, jnp.zeros((5, width), jnp.bfloat16)], axis=0
    )
    moved = lax.dot_general(
        parts, picks, (((1,), (1,)), ((), ())), preferred_element_type=jnp.float32
    )
    return ops, moved[0:1] + moved[1:2] + moved[2:3]


def newton(gram_matrix):
    identity = jnp.eye(gram_matrix.shape[0], dtype=jnp.float32)
    frobenius = jnp.sqrt(jnp.sum(gram_matrix * gram_matrix))
    scaled = gram_matrix / frobenius
    inverse_root = identity
    for repeat in range(NS_ITERS):
        factor = 1.5 * identity - 0.5 * jnp.dot(
            inverse_root, scaled, precision=lax.Precision.HIGHEST
        )
        scaled = jnp.dot(scaled, factor, precision=lax.Precision.HIGHEST)
        inverse_root = jnp.dot(factor, inverse_root, precision=lax.Precision.HIGHEST)
    return inverse_root.astype(jnp.bfloat16)


def doubling_sum(value):
    band_size = lax.axis_size("band")
    count = lax.axis_size("dom") * band_size
    bits = list(range(count.bit_length() - 1))
    order = bits[2:3] + bits[0:2] + bits[3:]
    total = value
    for bit in order:
        mask = 1 << bit
        pairs = [(i, i ^ mask) for i in range(count)]
        total = total + lax.ppermute(total, ("dom", "band"), pairs)
    return total


def body(states, cell_kinetic, cell_scale, cell_potential, connectivity, shared_nodes, cell_counts):
    left_face = shared_nodes[0, 0]
    right_face = shared_nodes[0, 1]
    face_width = left_face.shape[0]
    faces = jnp.concatenate([left_face, right_face])
    live_count = cell_counts[0]
    domain = lax.axis_index("dom")
    domains = lax.axis_size("dom")
    node_total = states.shape[1]
    state_cols = states.shape[0]
    has_left = (domain > 0).astype(jnp.float32)
    has_right = (domain < domains - 1).astype(jnp.float32)
    face_counts = jnp.concatenate(
        [jnp.full((face_width,), has_left), jnp.full((face_width,), has_right)]
    )
    node_weight = (
        jnp.ones((node_total,), jnp.float32)
        .at[faces]
        .set(1.0 / (1.0 + face_counts), unique_indices=True)
        .astype(jnp.bfloat16)
    )
    cells, width = connectivity.shape
    starts = jnp.arange(cells, dtype=jnp.int32) * (3 * (width // 4))
    slots = (connectivity - starts[:, None]) % node_total
    alive = (jnp.arange(cells) < live_count).astype(jnp.float32)
    scales = cell_scale * alive
    slot_rows = slots.reshape(cells, 1, width)
    potential_rows = (cell_potential * alive[:, None]).reshape(cells, 1, width)
    up = [(i, i + 1) for i in range(domains - 1)]
    down = [(j, i) for i, j in up]

    def exchange(left_values, right_values):
        from_left = lax.ppermute(right_values, "dom", up)
        from_right = lax.ppermute(left_values, "dom", down)
        return (from_left, from_right)

    first = states.T
    local_sum, *face_values, window_ops, window_pot = field_step(
        faces, scales, slot_rows, potential_rows, vector=first, kinetic=cell_kinetic
    )
    step = functools.partial(field_step, faces, scales, window_ops, window_pot)
    second, local_sum, *face_values = step(local_in=local_sum, received=exchange(*face_values))
    history = [first, second]
    for repeat in range(CHEB - 2):
        following, local_sum, *face_values = step(
            local_in=local_sum, received=exchange(*face_values), older=history[-2], alpha=2.0
        )
        history.append(following)
    (current,) = step(
        local_in=local_sum, received=exchange(*face_values), older=history[-2], alpha=2.0,
        apply=False,
    )
    row_shard = lax.all_to_all(current, "band", split_axis=0, concat_axis=1, tiled=True)
    piece_nodes = row_shard.shape[0]
    weight_rows = lax.dynamic_slice_in_dim(
        node_weight, lax.axis_index("band") * piece_nodes, piece_nodes, 0
    )
    weighted = row_shard * weight_rows[:, None]
    partial_gram = lax.dot_general(
        weighted, row_shard, (((0,), (0,)), ((), ())), preferred_element_type=jnp.float32
    )
    gram_matrix = doubling_sum(partial_gram)
    mixing = newton(gram_matrix)
    rotated = lax.dot_general(
        row_shard, mixing, (((1,), (0,)), ((), ())), preferred_element_type=jnp.float32
    ).astype(jnp.bfloat16)
    back = lax.all_to_all(rotated, "band", split_axis=1, concat_axis=0, tiled=True)
    return back.T


def solution(mesh):
    in_specs = (
        P("band", "dom"),
        P(),
        P("dom"),
        P("dom", None),
        P("dom", None),
        P("dom", None, None),
        P("dom"),
    )
    out_specs = P("band", "dom")
    return jax.shard_map(body, mesh=mesh, in_specs=in_specs, out_specs=out_specs, check_vma=False)
```

```python
import functools

import jax
import jax.numpy as jnp
from jax import lax
from jax.experimental import pallas as pl
from jax.experimental.pallas import tpu as pltpu
from jax.sharding import PartitionSpec as P

CHEB = 4
NS_ITERS = 5


VMEM_LIMIT = 60 * 1024 * 1024
BUILD_GROUP = 8
GROUP = 16


def field_kernel(combine, older, apply, build, alpha, group, *refs):
    refs = list(refs)
    faces = refs.pop(0)
    if apply:
        scales = refs.pop(0)
    if combine:
        local_in = refs.pop(0)
        received = (refs.pop(0), refs.pop(0))
        if older:
            older_ref = refs.pop(0)
    else:
        vector_in = refs.pop(0)
    if apply:
        ops_ref = refs.pop(0)
        pot_ref = refs.pop(0)
        if build:
            kinetic_ref = refs.pop(0)
    if combine:
        vector_out = refs.pop(0)
    if apply:
        local_out = refs.pop(0)
        faces_out = (refs.pop(0), refs.pop(0))
        if build:
            ops_out = refs.pop(0)
            pot_out = refs.pop(0)
    if combine:
        work = refs.pop(0)
    vector = vector_out if combine else vector_in
    face_half = faces.shape[0] // 2
    node_total = vector.shape[0]
    cell = pl.program_id(0) if apply else None

    def prologue():
        work[...] = local_in[...] if alpha == 1.0 else alpha * local_in[...]

        for side in range(2):
            def fix(p, carry):
                n = faces[side * face_half + p]
                row = received[side][pl.ds(p, 1), :]
                work[pl.ds(n, 1), :] += row if alpha == 1.0 else alpha * row
                return carry

            lax.fori_loop(0, face_half, fix, 0, unroll=8)
        value = work[...]
        if older:
            value = value - older_ref[...].astype(jnp.float32)
        vector_out[...] = value.astype(vector_out.dtype)

    if combine:
        if apply:
            pl.when(cell == 0)(prologue)
        else:
            prologue()

    if apply:
        width = ops_ref.shape[-1]
        quarter = width // 4
        body_rows = width - quarter

        @pl.when(cell == 0)
        def _():
            local_out[...] = jnp.zeros_like(local_out)

        for k in range(group):
            index = cell * group + k
            start = pl.multiple_of(index * body_rows, quarter)
            tail = pl.multiple_of(lax.rem((index + 1) * body_rows, node_total), quarter)
            main_rows = vector[pl.ds(start, body_rows), :]
            tail_rows = vector[pl.ds(tail, quarter), :]
            if build:
                ops, pot_row = build_operator(ops_ref[k], pot_ref[k], kinetic_ref[...])
                ops_out[k] = ops
                pot_out[k] = pot_row
            else:
                ops = ops_ref[k]
                pot_row = pot_ref[k]
            product = jnp.dot(ops[:, :body_rows], main_rows, preferred_element_type=jnp.float32)
            product = product + jnp.dot(
                ops[:, body_rows:], tail_rows, preferred_element_type=jnp.float32
            )
            scale = scales[index]
            pot = jnp.transpose(jnp.broadcast_to(pot_row, (8, width)))[:, 0:1]
            top = product[:body_rows] * scale + pot[:body_rows] * main_rows.astype(jnp.float32)
            bottom = product[body_rows:] * scale + pot[body_rows:] * tail_rows.astype(jnp.float32)
            local_out[pl.ds(start, body_rows), :] += top
            local_out[pl.ds(tail, quarter), :] += bottom

        @pl.when(cell == pl.num_programs(0) - 1)
        def _():
            for side in range(2):
                def pick(p, carry):
                    n = faces[side * face_half + p]
                    faces_out[side][pl.ds(p, 1), :] = local_out[pl.ds(n, 1), :]
                    return carry

                lax.fori_loop(0, face_half, pick, 0, unroll=8)


def field_step(faces, scales, window_ops, window_pot, vector=None, local_in=None,
               received=None, older=None, alpha=1.0, apply=True, kinetic=None):
    combine = local_in is not None
    has_older = older is not None
    build = kinetic is not None
    node_total, cols = (local_in if combine else vector).shape
    face_half = faces.shape[0] // 2
    cells, width = window_pot.shape[0], window_pot.shape[-1]
    smem = pl.BlockSpec(memory_space=pltpu.SMEM)
    whole = pl.BlockSpec(memory_space=pltpu.VMEM)
    args, specs = [faces], [smem]
    if apply:
        args.append(scales); specs.append(smem)
    if combine:
        args += [local_in, *received]; specs += [whole, whole, whole]
        if has_older:
            args.append(older); specs.append(whole)
    else:
        args.append(vector); specs.append(whole)
    group = BUILD_GROUP if build else GROUP
    cell_block = pl.BlockSpec((group, width, width), lambda c: (c, 0, 0))
    row_block = pl.BlockSpec((group, 1, width), lambda c: (c, 0, 0))
    if apply:
        args += [window_ops, window_pot]
        specs += [row_block if build else cell_block, row_block]
        if build:
            args.append(kinetic); specs.append(whole)
    out_shape, out_specs = [], []
    if combine:
        out_shape.append(jax.ShapeDtypeStruct((node_total, cols), jnp.bfloat16)); out_specs.append(whole)
    if apply:
        out_shape += [jax.ShapeDtypeStruct((node_total, cols), jnp.float32),
                      jax.ShapeDtypeStruct((face_half, cols), jnp.float32),
                      jax.ShapeDtypeStruct((face_half, cols), jnp.float32)]
        out_specs += [whole, whole, whole]
        if build:
            out_shape += [jax.ShapeDtypeStruct((cells, width, width), jnp.bfloat16),
                          jax.ShapeDtypeStruct((cells, 1, width), jnp.float32)]
            out_specs += [cell_block, row_block]
    scratch = [pltpu.VMEM((node_total, cols), jnp.float32)] if combine else []
    flops = (2 * cells * width * width * cols if apply else 0) + (4 * cells * width ** 3 if build else 0)
    result = pl.pallas_call(
        functools.partial(field_kernel, combine, has_older, apply, build, alpha, group),
        grid=(cells // group if apply else 1,),
        in_specs=specs,
        out_specs=out_specs,
        out_shape=out_shape,
        scratch_shapes=scratch,
        compiler_params=pltpu.CompilerParams(
            dimension_semantics=("arbitrary",), vmem_limit_bytes=VMEM_LIMIT),
        cost_estimate=pl.CostEstimate(
            flops=flops, transcendentals=0,
            bytes_accessed=(cells * width * width * 2 if apply else 0) + node_total * cols * 12),
    )(*args)
    return result


def build_operator(slot_row, pot_row, kinetic):
    width = kinetic.shape[0]
    picks = (lax.broadcasted_iota(jnp.int32, (width, width), 0) == slot_row).astype(jnp.bfloat16)
    columns = lax.dot_general(
        kinetic, picks, (((1,), (1,)), ((), ())), preferred_element_type=jnp.float32
    ).astype(jnp.bfloat16)
    ops = jnp.dot(picks, columns, preferred_element_type=jnp.float32).astype(jnp.bfloat16)
    high = pot_row.astype(jnp.bfloat16)
    rest = pot_row - high.astype(jnp.float32)
    middle = rest.astype(jnp.bfloat16)
    low = (rest - middle.astype(jnp.float32)).astype(jnp.bfloat16)
    parts = jnp.concatenate(
        [high, middle, low, jnp.zeros((5, width), jnp.bfloat16)], axis=0
    )
    moved = lax.dot_general(
        parts, picks, (((1,), (1,)), ((), ())), preferred_element_type=jnp.float32
    )
    return ops, moved[0:1] + moved[1:2] + moved[2:3]


def newton(gram_matrix):
    identity = jnp.eye(gram_matrix.shape[0], dtype=jnp.float32)
    frobenius = jnp.sqrt(jnp.sum(gram_matrix * gram_matrix))
    scaled = gram_matrix / frobenius
    inverse_root = identity
    for repeat in range(NS_ITERS):
        factor = 1.5 * identity - 0.5 * jnp.dot(
            inverse_root, scaled, precision=lax.Precision.HIGHEST
        )
        scaled = jnp.dot(scaled, factor, precision=lax.Precision.HIGHEST)
        inverse_root = jnp.dot(factor, inverse_root, precision=lax.Precision.HIGHEST)
    return inverse_root.astype(jnp.bfloat16)


def doubling_sum(value):
    band_size = lax.axis_size("band")
    count = lax.axis_size("dom") * band_size
    bits = list(range(count.bit_length() - 1))
    order = bits[2:3] + bits[0:2] + bits[3:]
    total = value
    for bit in order:
        mask = 1 << bit
        pairs = [(i, i ^ mask) for i in range(count)]
        total = total + lax.ppermute(total, ("dom", "band"), pairs)
    return total


def body(states, cell_kinetic, cell_scale, cell_potential, connectivity, shared_nodes, cell_counts):
    left_face = shared_nodes[0, 0]
    right_face = shared_nodes[0, 1]
    face_width = left_face.shape[0]
    faces = jnp.concatenate([left_face, right_face])
    live_count = cell_counts[0]
    domain = lax.axis_index("dom")
    domains = lax.axis_size("dom")
    node_total = states.shape[1]
    state_cols = states.shape[0]
    has_left = (domain > 0).astype(jnp.float32)
    has_right = (domain < domains - 1).astype(jnp.float32)
    face_counts = jnp.concatenate(
        [jnp.full((face_width,), has_left), jnp.full((face_width,), has_right)]
    )
    node_weight = (
        jnp.ones((node_total,), jnp.float32)
        .at[faces]
        .set(1.0 / (1.0 + face_counts), unique_indices=True)
        .astype(jnp.bfloat16)
    )
    cells, width = connectivity.shape
    starts = jnp.arange(cells, dtype=jnp.int32) * (3 * (width // 4))
    slots = (connectivity - starts[:, None]) % node_total
    alive = (jnp.arange(cells) < live_count).astype(jnp.float32)
    scales = cell_scale * alive
    slot_rows = slots.reshape(cells, 1, width)
    potential_rows = (cell_potential * alive[:, None]).reshape(cells, 1, width)
    up = [(i, i + 1) for i in range(domains - 1)]
    down = [(j, i) for i, j in up]

    def exchange(left_values, right_values):
        from_left = lax.ppermute(right_values, "dom", up)
        from_right = lax.ppermute(left_values, "dom", down)
        return (from_left, from_right)

    first = states.T
    local_sum, *face_values, window_ops, window_pot = field_step(
        faces, scales, slot_rows, potential_rows, vector=first, kinetic=cell_kinetic
    )
    step = functools.partial(field_step, faces, scales, window_ops, window_pot)
    second, local_sum, *face_values = step(local_in=local_sum, received=exchange(*face_values))
    history = [first, second]
    for repeat in range(CHEB - 2):
        following, local_sum, *face_values = step(
            local_in=local_sum, received=exchange(*face_values), older=history[-2], alpha=2.0
        )
        history.append(following)
    (current,) = step(
        local_in=local_sum, received=exchange(*face_values), older=history[-2], alpha=2.0,
        apply=False,
    )
    row_shard = lax.all_to_all(current, "band", split_axis=0, concat_axis=1, tiled=True)
    piece_nodes = row_shard.shape[0]
    weight_rows = lax.dynamic_slice_in_dim(
        node_weight, lax.axis_index("band") * piece_nodes, piece_nodes, 0
    )
    weighted = row_shard * weight_rows[:, None]
    partial_gram = lax.dot_general(
        weighted, row_shard, (((0,), (0,)), ((), ())), preferred_element_type=jnp.float32
    )
    gram_matrix = doubling_sum(partial_gram)
    mixing = newton(gram_matrix)
    rotated = lax.dot_general(
        row_shard, mixing, (((1,), (0,)), ((), ())), preferred_element_type=jnp.float32
    ).astype(jnp.bfloat16)
    back = lax.all_to_all(rotated, "band", split_axis=1, concat_axis=0, tiled=True)
    return back.T


def solution(mesh):
    in_specs = (
        P("band", "dom"),
        P(),
        P("dom"),
        P("dom", None),
        P("dom", None),
        P("dom", None, None),
        P("dom"),
    )
    out_specs = P("band", "dom")
    return jax.shard_map(body, mesh=mesh, in_specs=in_specs, out_specs=out_specs, check_vma=False)
```

```python
import functools

import jax
import jax.numpy as jnp
from jax import lax
from jax.experimental import pallas as pl
from jax.experimental.pallas import tpu as pltpu
from jax.sharding import PartitionSpec as P

CHEB = 4
NS_ITERS = 5


VMEM_LIMIT = 60 * 1024 * 1024
BUILD_GROUP = 16
GROUP = 16


def field_kernel(combine, older, apply, build, alpha, group, *refs):
    refs = list(refs)
    faces = refs.pop(0)
    if apply:
        scales = refs.pop(0)
    if combine:
        local_in = refs.pop(0)
        received = (refs.pop(0), refs.pop(0))
        if older:
            older_ref = refs.pop(0)
    else:
        vector_in = refs.pop(0)
    if apply:
        ops_ref = refs.pop(0)
        pot_ref = refs.pop(0)
        if build:
            kinetic_ref = refs.pop(0)
    if combine:
        vector_out = refs.pop(0)
    if apply:
        local_out = refs.pop(0)
        faces_out = (refs.pop(0), refs.pop(0))
        if build:
            ops_out = refs.pop(0)
            pot_out = refs.pop(0)
    if combine:
        work = refs.pop(0)
    vector = vector_out if combine else vector_in
    face_half = faces.shape[0] // 2
    node_total = vector.shape[0]
    cell = pl.program_id(0) if apply else None

    def prologue():
        work[...] = local_in[...] if alpha == 1.0 else alpha * local_in[...]

        for side in range(2):
            def fix(p, carry):
                n = faces[side * face_half + p]
                row = received[side][pl.ds(p, 1), :]
                work[pl.ds(n, 1), :] += row if alpha == 1.0 else alpha * row
                return carry

            lax.fori_loop(0, face_half, fix, 0, unroll=8)
        value = work[...]
        if older:
            value = value - older_ref[...].astype(jnp.float32)
        vector_out[...] = value.astype(vector_out.dtype)

    if combine:
        if apply:
            pl.when(cell == 0)(prologue)
        else:
            prologue()

    if apply:
        width = ops_ref.shape[-1]
        quarter = width // 4
        body_rows = width - quarter

        @pl.when(cell == 0)
        def _():
            local_out[...] = jnp.zeros_like(local_out)

        for k in range(group):
            index = cell * group + k
            start = pl.multiple_of(index * body_rows, quarter)
            tail = pl.multiple_of(lax.rem((index + 1) * body_rows, node_total), quarter)
            main_rows = vector[pl.ds(start, body_rows), :]
            tail_rows = vector[pl.ds(tail, quarter), :]
            if build:
                ops, pot_row = build_operator(ops_ref[k], pot_ref[k], kinetic_ref[...])
                ops_out[k] = ops
                pot_out[k] = pot_row
            else:
                ops = ops_ref[k]
                pot_row = pot_ref[k]
            product = jnp.dot(ops[:, :body_rows], main_rows, preferred_element_type=jnp.float32)
            product = product + jnp.dot(
                ops[:, body_rows:], tail_rows, preferred_element_type=jnp.float32
            )
            scale = scales[index]
            pot = jnp.transpose(jnp.broadcast_to(pot_row, (8, width)))[:, 0:1]
            top = product[:body_rows] * scale + pot[:body_rows] * main_rows.astype(jnp.float32)
            bottom = product[body_rows:] * scale + pot[body_rows:] * tail_rows.astype(jnp.float32)
            local_out[pl.ds(start, body_rows), :] += top
            local_out[pl.ds(tail, quarter), :] += bottom

        @pl.when(cell == pl.num_programs(0) - 1)
        def _():
            for side in range(2):
                def pick(p, carry):
                    n = faces[side * face_half + p]
                    faces_out[side][pl.ds(p, 1), :] = local_out[pl.ds(n, 1), :]
                    return carry

                lax.fori_loop(0, face_half, pick, 0, unroll=8)


def field_step(faces, scales, window_ops, window_pot, vector=None, local_in=None,
               received=None, older=None, alpha=1.0, apply=True, kinetic=None):
    combine = local_in is not None
    has_older = older is not None
    build = kinetic is not None
    node_total, cols = (local_in if combine else vector).shape
    face_half = faces.shape[0] // 2
    cells, width = window_pot.shape[0], window_pot.shape[-1]
    smem = pl.BlockSpec(memory_space=pltpu.SMEM)
    whole = pl.BlockSpec(memory_space=pltpu.VMEM)
    args, specs = [faces], [smem]
    if apply:
        args.append(scales); specs.append(smem)
    if combine:
        args += [local_in, *received]; specs += [whole, whole, whole]
        if has_older:
            args.append(older); specs.append(whole)
    else:
        args.append(vector); specs.append(whole)
    group = BUILD_GROUP if build else GROUP
    cell_block = pl.BlockSpec((group, width, width), lambda c: (c, 0, 0))
    row_block = pl.BlockSpec((group, 1, width), lambda c: (c, 0, 0))
    if apply:
        args += [window_ops, window_pot]
        specs += [row_block if build else cell_block, row_block]
        if build:
            args.append(kinetic); specs.append(whole)
    out_shape, out_specs = [], []
    if combine:
        out_shape.append(jax.ShapeDtypeStruct((node_total, cols), jnp.bfloat16)); out_specs.append(whole)
    if apply:
        out_shape += [jax.ShapeDtypeStruct((node_total, cols), jnp.float32),
                      jax.ShapeDtypeStruct((face_half, cols), jnp.float32),
                      jax.ShapeDtypeStruct((face_half, cols), jnp.float32)]
        out_specs += [whole, whole, whole]
        if build:
            out_shape += [jax.ShapeDtypeStruct((cells, width, width), jnp.bfloat16),
                          jax.ShapeDtypeStruct((cells, 1, width), jnp.float32)]
            out_specs += [cell_block, row_block]
    scratch = [pltpu.VMEM((node_total, cols), jnp.float32)] if combine else []
    flops = (2 * cells * width * width * cols if apply else 0) + (4 * cells * width ** 3 if build else 0)
    result = pl.pallas_call(
        functools.partial(field_kernel, combine, has_older, apply, build, alpha, group),
        grid=(cells // group if apply else 1,),
        in_specs=specs,
        out_specs=out_specs,
        out_shape=out_shape,
        scratch_shapes=scratch,
        compiler_params=pltpu.CompilerParams(
            dimension_semantics=("arbitrary",), vmem_limit_bytes=VMEM_LIMIT),
        cost_estimate=pl.CostEstimate(
            flops=flops, transcendentals=0,
            bytes_accessed=(cells * width * width * 2 if apply else 0) + node_total * cols * 12),
    )(*args)
    return result


def build_operator(slot_row, pot_row, kinetic):
    width = kinetic.shape[0]
    picks = (lax.broadcasted_iota(jnp.int32, (width, width), 0) == slot_row).astype(jnp.bfloat16)
    columns = lax.dot_general(
        kinetic, picks, (((1,), (1,)), ((), ())), preferred_element_type=jnp.float32
    ).astype(jnp.bfloat16)
    ops = jnp.dot(picks, columns, preferred_element_type=jnp.float32).astype(jnp.bfloat16)
    high = pot_row.astype(jnp.bfloat16)
    rest = pot_row - high.astype(jnp.float32)
    middle = rest.astype(jnp.bfloat16)
    low = (rest - middle.astype(jnp.float32)).astype(jnp.bfloat16)
    parts = jnp.concatenate(
        [high, middle, low, jnp.zeros((5, width), jnp.bfloat16)], axis=0
    )
    moved = lax.dot_general(
        parts, picks, (((1,), (1,)), ((), ())), preferred_element_type=jnp.float32
    )
    return ops, moved[0:1] + moved[1:2] + moved[2:3]


def newton(gram_matrix):
    identity = jnp.eye(gram_matrix.shape[0], dtype=jnp.float32)
    frobenius = jnp.sqrt(jnp.sum(gram_matrix * gram_matrix))
    scaled = gram_matrix / frobenius
    inverse_root = identity
    for repeat in range(NS_ITERS):
        factor = 1.5 * identity - 0.5 * jnp.dot(
            inverse_root, scaled, precision=lax.Precision.HIGHEST
        )
        scaled = jnp.dot(scaled, factor, precision=lax.Precision.HIGHEST)
        inverse_root = jnp.dot(factor, inverse_root, precision=lax.Precision.HIGHEST)
    return inverse_root.astype(jnp.bfloat16)


def doubling_sum(value):
    band_size = lax.axis_size("band")
    count = lax.axis_size("dom") * band_size
    bits = list(range(count.bit_length() - 1))
    order = bits[2:3] + bits[0:2] + bits[3:]
    total = value
    for bit in order:
        mask = 1 << bit
        pairs = [(i, i ^ mask) for i in range(count)]
        total = total + lax.ppermute(total, ("dom", "band"), pairs)
    return total


def body(states, cell_kinetic, cell_scale, cell_potential, connectivity, shared_nodes, cell_counts):
    left_face = shared_nodes[0, 0]
    right_face = shared_nodes[0, 1]
    face_width = left_face.shape[0]
    faces = jnp.concatenate([left_face, right_face])
    live_count = cell_counts[0]
    domain = lax.axis_index("dom")
    domains = lax.axis_size("dom")
    node_total = states.shape[1]
    state_cols = states.shape[0]
    has_left = (domain > 0).astype(jnp.float32)
    has_right = (domain < domains - 1).astype(jnp.float32)
    face_counts = jnp.concatenate(
        [jnp.full((face_width,), has_left), jnp.full((face_width,), has_right)]
    )
    node_weight = (
        jnp.ones((node_total,), jnp.float32)
        .at[faces]
        .set(1.0 / (1.0 + face_counts), unique_indices=True)
        .astype(jnp.bfloat16)
    )
    cells, width = connectivity.shape
    starts = jnp.arange(cells, dtype=jnp.int32) * (3 * (width // 4))
    slots = (connectivity - starts[:, None]) % node_total
    alive = (jnp.arange(cells) < live_count).astype(jnp.float32)
    scales = cell_scale * alive
    slot_rows = slots.reshape(cells, 1, width)
    potential_rows = (cell_potential * alive[:, None]).reshape(cells, 1, width)
    up = [(i, i + 1) for i in range(domains - 1)]
    down = [(j, i) for i, j in up]

    def exchange(left_values, right_values):
        from_left = lax.ppermute(right_values, "dom", up)
        from_right = lax.ppermute(left_values, "dom", down)
        return (from_left, from_right)

    first = states.T
    local_sum, *face_values, window_ops, window_pot = field_step(
        faces, scales, slot_rows, potential_rows, vector=first, kinetic=cell_kinetic
    )
    step = functools.partial(field_step, faces, scales, window_ops, window_pot)
    second, local_sum, *face_values = step(local_in=local_sum, received=exchange(*face_values))
    history = [first, second]
    for repeat in range(CHEB - 2):
        following, local_sum, *face_values = step(
            local_in=local_sum, received=exchange(*face_values), older=history[-2], alpha=2.0
        )
        history.append(following)
    (current,) = step(
        local_in=local_sum, received=exchange(*face_values), older=history[-2], alpha=2.0,
        apply=False,
    )
    row_shard = lax.all_to_all(current, "band", split_axis=0, concat_axis=1, tiled=True)
    piece_nodes = row_shard.shape[0]
    weight_rows = lax.dynamic_slice_in_dim(
        node_weight, lax.axis_index("band") * piece_nodes, piece_nodes, 0
    )
    weighted = row_shard * weight_rows[:, None]
    partial_gram = lax.dot_general(
        weighted, row_shard, (((0,), (0,)), ((), ())), preferred_element_type=jnp.float32
    )
    gram_matrix = doubling_sum(partial_gram)
    mixing = newton(gram_matrix)
    rotated = lax.dot_general(
        row_shard, mixing, (((1,), (0,)), ((), ())), preferred_element_type=jnp.float32
    ).astype(jnp.bfloat16)
    back = lax.all_to_all(rotated, "band", split_axis=1, concat_axis=0, tiled=True)
    return back.T


def solution(mesh):
    in_specs = (
        P("band", "dom"),
        P(),
        P("dom"),
        P("dom", None),
        P("dom", None),
        P("dom", None, None),
        P("dom"),
    )
    out_specs = P("band", "dom")
    return jax.shard_map(body, mesh=mesh, in_specs=in_specs, out_specs=out_specs, check_vma=False)
```

```python
import functools

import jax
import jax.numpy as jnp
from jax import lax
from jax.experimental import pallas as pl
from jax.experimental.pallas import tpu as pltpu
from jax.sharding import PartitionSpec as P

CHEB = 4
NS_ITERS = 5


VMEM_LIMIT = 60 * 1024 * 1024
BUILD_GROUP = 8
GROUP = 16


def field_kernel(combine, older, apply, build, alpha, group, *refs):
    refs = list(refs)
    faces = refs.pop(0)
    if apply:
        scales = refs.pop(0)
    if combine:
        local_in = refs.pop(0)
        received = (refs.pop(0), refs.pop(0))
        if older:
            older_ref = refs.pop(0)
    else:
        vector_in = refs.pop(0)
    if apply:
        ops_ref = refs.pop(0)
        pot_ref = refs.pop(0)
        if build:
            kinetic_ref = refs.pop(0)
    if combine:
        vector_out = refs.pop(0)
    if apply:
        local_out = refs.pop(0)
        faces_out = (refs.pop(0), refs.pop(0))
        if build:
            ops_out = refs.pop(0)
            pot_out = refs.pop(0)
    if combine:
        work = refs.pop(0)
    vector = vector_out if combine else vector_in
    face_half = faces.shape[0] // 2
    node_total = vector.shape[0]
    cell = pl.program_id(0) if apply else None

    def prologue():
        work[...] = local_in[...] if alpha == 1.0 else alpha * local_in[...]

        for side in range(2):
            def fix(p, carry):
                n = faces[side * face_half + p]
                row = received[side][pl.ds(p, 1), :]
                work[pl.ds(n, 1), :] += row if alpha == 1.0 else alpha * row
                return carry

            lax.fori_loop(0, face_half, fix, 0, unroll=16)
        value = work[...]
        if older:
            value = value - older_ref[...].astype(jnp.float32)
        vector_out[...] = value.astype(vector_out.dtype)

    if combine:
        if apply:
            pl.when(cell == 0)(prologue)
        else:
            prologue()

    if apply:
        width = ops_ref.shape[-1]
        quarter = width // 4
        body_rows = width - quarter

        @pl.when(cell == 0)
        def _():
            local_out[...] = jnp.zeros_like(local_out)

        for k in range(group):
            index = cell * group + k
            start = pl.multiple_of(index * body_rows, quarter)
            tail = pl.multiple_of(lax.rem((index + 1) * body_rows, node_total), quarter)
            main_rows = vector[pl.ds(start, body_rows), :]
            tail_rows = vector[pl.ds(tail, quarter), :]
            if build:
                ops, pot_row = build_operator(ops_ref[k], pot_ref[k], kinetic_ref[...])
                ops_out[k] = ops
                pot_out[k] = pot_row
            else:
                ops = ops_ref[k]
                pot_row = pot_ref[k]
            product = jnp.dot(ops[:, :body_rows], main_rows, preferred_element_type=jnp.float32)
            product = product + jnp.dot(
                ops[:, body_rows:], tail_rows, preferred_element_type=jnp.float32
            )
            scale = scales[index]
            pot = jnp.transpose(jnp.broadcast_to(pot_row, (8, width)))[:, 0:1]
            top = product[:body_rows] * scale + pot[:body_rows] * main_rows.astype(jnp.float32)
            bottom = product[body_rows:] * scale + pot[body_rows:] * tail_rows.astype(jnp.float32)
            local_out[pl.ds(start, body_rows), :] += top
            local_out[pl.ds(tail, quarter), :] += bottom

        @pl.when(cell == pl.num_programs(0) - 1)
        def _():
            for side in range(2):
                def pick(p, carry):
                    n = faces[side * face_half + p]
                    faces_out[side][pl.ds(p, 1), :] = local_out[pl.ds(n, 1), :]
                    return carry

                lax.fori_loop(0, face_half, pick, 0, unroll=16)


def field_step(faces, scales, window_ops, window_pot, vector=None, local_in=None,
               received=None, older=None, alpha=1.0, apply=True, kinetic=None):
    combine = local_in is not None
    has_older = older is not None
    build = kinetic is not None
    node_total, cols = (local_in if combine else vector).shape
    face_half = faces.shape[0] // 2
    cells, width = window_pot.shape[0], window_pot.shape[-1]
    smem = pl.BlockSpec(memory_space=pltpu.SMEM)
    whole = pl.BlockSpec(memory_space=pltpu.VMEM)
    args, specs = [faces], [smem]
    if apply:
        args.append(scales); specs.append(smem)
    if combine:
        args += [local_in, *received]; specs += [whole, whole, whole]
        if has_older:
            args.append(older); specs.append(whole)
    else:
        args.append(vector); specs.append(whole)
    group = BUILD_GROUP if build else GROUP
    cell_block = pl.BlockSpec((group, width, width), lambda c: (c, 0, 0))
    row_block = pl.BlockSpec((group, 1, width), lambda c: (c, 0, 0))
    if apply:
        args += [window_ops, window_pot]
        specs += [row_block if build else cell_block, row_block]
        if build:
            args.append(kinetic); specs.append(whole)
    out_shape, out_specs = [], []
    if combine:
        out_shape.append(jax.ShapeDtypeStruct((node_total, cols), jnp.bfloat16)); out_specs.append(whole)
    if apply:
        out_shape += [jax.ShapeDtypeStruct((node_total, cols), jnp.float32),
                      jax.ShapeDtypeStruct((face_half, cols), jnp.float32),
                      jax.ShapeDtypeStruct((face_half, cols), jnp.float32)]
        out_specs += [whole, whole, whole]
        if build:
            out_shape += [jax.ShapeDtypeStruct((cells, width, width), jnp.bfloat16),
                          jax.ShapeDtypeStruct((cells, 1, width), jnp.float32)]
            out_specs += [cell_block, row_block]
    scratch = [pltpu.VMEM((node_total, cols), jnp.float32)] if combine else []
    flops = (2 * cells * width * width * cols if apply else 0) + (4 * cells * width ** 3 if build else 0)
    result = pl.pallas_call(
        functools.partial(field_kernel, combine, has_older, apply, build, alpha, group),
        grid=(cells // group if apply else 1,),
        in_specs=specs,
        out_specs=out_specs,
        out_shape=out_shape,
        scratch_shapes=scratch,
        compiler_params=pltpu.CompilerParams(
            dimension_semantics=("arbitrary",), vmem_limit_bytes=VMEM_LIMIT),
        cost_estimate=pl.CostEstimate(
            flops=flops, transcendentals=0,
            bytes_accessed=(cells * width * width * 2 if apply else 0) + node_total * cols * 12),
    )(*args)
    return result


def build_operator(slot_row, pot_row, kinetic):
    width = kinetic.shape[0]
    picks = (lax.broadcasted_iota(jnp.int32, (width, width), 0) == slot_row).astype(jnp.bfloat16)
    columns = lax.dot_general(
        kinetic, picks, (((1,), (1,)), ((), ())), preferred_element_type=jnp.float32
    ).astype(jnp.bfloat16)
    ops = jnp.dot(picks, columns, preferred_element_type=jnp.float32).astype(jnp.bfloat16)
    high = pot_row.astype(jnp.bfloat16)
    rest = pot_row - high.astype(jnp.float32)
    middle = rest.astype(jnp.bfloat16)
    low = (rest - middle.astype(jnp.float32)).astype(jnp.bfloat16)
    parts = jnp.concatenate(
        [high, middle, low, jnp.zeros((5, width), jnp.bfloat16)], axis=0
    )
    moved = lax.dot_general(
        parts, picks, (((1,), (1,)), ((), ())), preferred_element_type=jnp.float32
    )
    return ops, moved[0:1] + moved[1:2] + moved[2:3]


def newton(gram_matrix):
    identity = jnp.eye(gram_matrix.shape[0], dtype=jnp.float32)
    frobenius = jnp.sqrt(jnp.sum(gram_matrix * gram_matrix))
    scaled = gram_matrix / frobenius
    inverse_root = identity
    for repeat in range(NS_ITERS):
        factor = 1.5 * identity - 0.5 * jnp.dot(
            inverse_root, scaled, precision=lax.Precision.HIGHEST
        )
        scaled = jnp.dot(scaled, factor, precision=lax.Precision.HIGHEST)
        inverse_root = jnp.dot(factor, inverse_root, precision=lax.Precision.HIGHEST)
    return inverse_root.astype(jnp.bfloat16)


def doubling_sum(value):
    band_size = lax.axis_size("band")
    count = lax.axis_size("dom") * band_size
    bits = list(range(count.bit_length() - 1))
    order = bits[2:3] + bits[0:2] + bits[3:]
    total = value
    for bit in order:
        mask = 1 << bit
        pairs = [(i, i ^ mask) for i in range(count)]
        total = total + lax.ppermute(total, ("dom", "band"), pairs)
    return total


def body(states, cell_kinetic, cell_scale, cell_potential, connectivity, shared_nodes, cell_counts):
    left_face = shared_nodes[0, 0]
    right_face = shared_nodes[0, 1]
    face_width = left_face.shape[0]
    faces = jnp.concatenate([left_face, right_face])
    live_count = cell_counts[0]
    domain = lax.axis_index("dom")
    domains = lax.axis_size("dom")
    node_total = states.shape[1]
    state_cols = states.shape[0]
    has_left = (domain > 0).astype(jnp.float32)
    has_right = (domain < domains - 1).astype(jnp.float32)
    face_counts = jnp.concatenate(
        [jnp.full((face_width,), has_left), jnp.full((face_width,), has_right)]
    )
    node_weight = (
        jnp.ones((node_total,), jnp.float32)
        .at[faces]
        .set(1.0 / (1.0 + face_counts), unique_indices=True)
        .astype(jnp.bfloat16)
    )
    cells, width = connectivity.shape
    starts = jnp.arange(cells, dtype=jnp.int32) * (3 * (width // 4))
    slots = (connectivity - starts[:, None]) % node_total
    alive = (jnp.arange(cells) < live_count).astype(jnp.float32)
    scales = cell_scale * alive
    slot_rows = slots.reshape(cells, 1, width)
    potential_rows = (cell_potential * alive[:, None]).reshape(cells, 1, width)
    up = [(i, i + 1) for i in range(domains - 1)]
    down = [(j, i) for i, j in up]

    def exchange(left_values, right_values):
        from_left = lax.ppermute(right_values, "dom", up)
        from_right = lax.ppermute(left_values, "dom", down)
        return (from_left, from_right)

    first = states.T
    local_sum, *face_values, window_ops, window_pot = field_step(
        faces, scales, slot_rows, potential_rows, vector=first, kinetic=cell_kinetic
    )
    step = functools.partial(field_step, faces, scales, window_ops, window_pot)
    second, local_sum, *face_values = step(local_in=local_sum, received=exchange(*face_values))
    history = [first, second]
    for repeat in range(CHEB - 2):
        following, local_sum, *face_values = step(
            local_in=local_sum, received=exchange(*face_values), older=history[-2], alpha=2.0
        )
        history.append(following)
    (current,) = step(
        local_in=local_sum, received=exchange(*face_values), older=history[-2], alpha=2.0,
        apply=False,
    )
    row_shard = lax.all_to_all(current, "band", split_axis=0, concat_axis=1, tiled=True)
    piece_nodes = row_shard.shape[0]
    weight_rows = lax.dynamic_slice_in_dim(
        node_weight, lax.axis_index("band") * piece_nodes, piece_nodes, 0
    )
    weighted = row_shard * weight_rows[:, None]
    partial_gram = lax.dot_general(
        weighted, row_shard, (((0,), (0,)), ((), ())), preferred_element_type=jnp.float32
    )
    gram_matrix = doubling_sum(partial_gram)
    mixing = newton(gram_matrix)
    rotated = lax.dot_general(
        row_shard, mixing, (((1,), (0,)), ((), ())), preferred_element_type=jnp.float32
    ).astype(jnp.bfloat16)
    back = lax.all_to_all(rotated, "band", split_axis=1, concat_axis=0, tiled=True)
    return back.T


def solution(mesh):
    in_specs = (
        P("band", "dom"),
        P(),
        P("dom"),
        P("dom", None),
        P("dom", None),
        P("dom", None, None),
        P("dom"),
    )
    out_specs = P("band", "dom")
    return jax.shard_map(body, mesh=mesh, in_specs=in_specs, out_specs=out_specs, check_vma=False)
```

```python
import functools

import jax
import jax.numpy as jnp
from jax import lax
from jax.experimental import pallas as pl
from jax.experimental.pallas import tpu as pltpu
from jax.sharding import PartitionSpec as P

CHEB = 4
NS_ITERS = 5


VMEM_LIMIT = 60 * 1024 * 1024
BUILD_GROUP = 8
GROUP = 16


def field_kernel(combine, older, apply, build, alpha, group, *refs):
    refs = list(refs)
    faces = refs.pop(0)
    if apply:
        scales = refs.pop(0)
    if combine:
        local_in = refs.pop(0)
        received = (refs.pop(0), refs.pop(0))
        if older:
            older_ref = refs.pop(0)
    else:
        vector_in = refs.pop(0)
    if apply:
        ops_ref = refs.pop(0)
        pot_ref = refs.pop(0)
        if build:
            kinetic_ref = refs.pop(0)
    if combine:
        vector_out = refs.pop(0)
    if apply:
        local_out = refs.pop(0)
        faces_out = (refs.pop(0), refs.pop(0))
        if build:
            ops_out = refs.pop(0)
            pot_out = refs.pop(0)
    if combine:
        work = refs.pop(0)
    vector = vector_out if combine else vector_in
    face_half = faces.shape[0] // 2
    node_total = vector.shape[0]
    cell = pl.program_id(0) if apply else None

    def prologue():
        work[...] = local_in[...] if alpha == 1.0 else alpha * local_in[...]

        for side in range(2):
            def fix(p, carry):
                n = faces[side * face_half + p]
                row = received[side][pl.ds(p, 1), :]
                work[pl.ds(n, 1), :] += row if alpha == 1.0 else alpha * row
                return carry

            lax.fori_loop(0, face_half, fix, 0, unroll=8)
        value = work[...]
        if older:
            value = value - older_ref[...].astype(jnp.float32)
        vector_out[...] = value.astype(vector_out.dtype)

    if combine:
        if apply:
            pl.when(cell == 0)(prologue)
        else:
            prologue()

    if apply:
        width = ops_ref.shape[-1]
        quarter = width // 4
        body_rows = width - quarter

        @pl.when(cell == 0)
        def _():
            local_out[...] = jnp.zeros_like(local_out)

        for k in range(group):
            index = cell * group + k
            start = pl.multiple_of(index * body_rows, quarter)
            tail = pl.multiple_of(lax.rem((index + 1) * body_rows, node_total), quarter)
            main_rows = vector[pl.ds(start, body_rows), :]
            tail_rows = vector[pl.ds(tail, quarter), :]
            if build:
                ops, pot_row = build_operator(ops_ref[k], pot_ref[k], kinetic_ref[...])
                ops_out[k] = ops
                pot_out[k] = pot_row
            else:
                ops = ops_ref[k]
                pot_row = pot_ref[k]
            product = jnp.dot(ops[:, :body_rows], main_rows, preferred_element_type=jnp.float32)
            product = product + jnp.dot(
                ops[:, body_rows:], tail_rows, preferred_element_type=jnp.float32
            )
            scale = scales[index]
            pot = jnp.transpose(jnp.broadcast_to(pot_row, (8, width)))[:, 0:1]
            top = product[:body_rows] * scale + pot[:body_rows] * main_rows.astype(jnp.float32)
            bottom = product[body_rows:] * scale + pot[body_rows:] * tail_rows.astype(jnp.float32)
            local_out[pl.ds(start, body_rows), :] += top
            local_out[pl.ds(tail, quarter), :] += bottom

        @pl.when(cell == pl.num_programs(0) - 1)
        def _():
            for side in range(2):
                def pick(p, carry):
                    n = faces[side * face_half + p]
                    faces_out[side][pl.ds(p, 1), :] = local_out[pl.ds(n, 1), :]
                    return carry

                lax.fori_loop(0, face_half, pick, 0, unroll=8)


def field_step(faces, scales, window_ops, window_pot, vector=None, local_in=None,
               received=None, older=None, alpha=1.0, apply=True, kinetic=None):
    combine = local_in is not None
    has_older = older is not None
    build = kinetic is not None
    node_total, cols = (local_in if combine else vector).shape
    face_half = faces.shape[0] // 2
    cells, width = window_pot.shape[0], window_pot.shape[-1]
    smem = pl.BlockSpec(memory_space=pltpu.SMEM)
    whole = pl.BlockSpec(memory_space=pltpu.VMEM)
    args, specs = [faces], [smem]
    if apply:
        args.append(scales); specs.append(smem)
    if combine:
        args += [local_in, *received]; specs += [whole, whole, whole]
        if has_older:
            args.append(older); specs.append(whole)
    else:
        args.append(vector); specs.append(whole)
    group = BUILD_GROUP if build else GROUP
    cell_block = pl.BlockSpec((group, width, width), lambda c: (c, 0, 0))
    row_block = pl.BlockSpec((group, 1, width), lambda c: (c, 0, 0))
    if apply:
        args += [window_ops, window_pot]
        specs += [row_block if build else cell_block, row_block]
        if build:
            args.append(kinetic); specs.append(whole)
    out_shape, out_specs = [], []
    if combine:
        out_shape.append(jax.ShapeDtypeStruct((node_total, cols), jnp.bfloat16)); out_specs.append(whole)
    if apply:
        out_shape += [jax.ShapeDtypeStruct((node_total, cols), jnp.float32),
                      jax.ShapeDtypeStruct((face_half, cols), jnp.float32),
                      jax.ShapeDtypeStruct((face_half, cols), jnp.float32)]
        out_specs += [whole, whole, whole]
        if build:
            out_shape += [jax.ShapeDtypeStruct((cells, width, width), jnp.bfloat16),
                          jax.ShapeDtypeStruct((cells, 1, width), jnp.float32)]
            out_specs += [cell_block, row_block]
    scratch = [pltpu.VMEM((node_total, cols), jnp.float32)] if combine else []
    flops = (2 * cells * width * width * cols if apply else 0) + (4 * cells * width ** 3 if build else 0)
    result = pl.pallas_call(
        functools.partial(field_kernel, combine, has_older, apply, build, alpha, group),
        grid=(cells // group if apply else 1,),
        in_specs=specs,
        out_specs=out_specs,
        out_shape=out_shape,
        scratch_shapes=scratch,
        compiler_params=pltpu.CompilerParams(
            dimension_semantics=("arbitrary",), vmem_limit_bytes=VMEM_LIMIT),
        cost_estimate=pl.CostEstimate(
            flops=flops, transcendentals=0,
            bytes_accessed=(cells * width * width * 2 if apply else 0) + node_total * cols * 12),
    )(*args)
    return result


def build_operator(slot_row, pot_row, kinetic):
    width = kinetic.shape[0]
    picks = (lax.broadcasted_iota(jnp.int32, (width, width), 0) == slot_row).astype(jnp.bfloat16)
    columns = lax.dot_general(
        kinetic, picks, (((1,), (1,)), ((), ())), preferred_element_type=jnp.float32
    ).astype(jnp.bfloat16)
    ops = jnp.dot(picks, columns, preferred_element_type=jnp.float32).astype(jnp.bfloat16)
    high = pot_row.astype(jnp.bfloat16)
    rest = pot_row - high.astype(jnp.float32)
    middle = rest.astype(jnp.bfloat16)
    low = (rest - middle.astype(jnp.float32)).astype(jnp.bfloat16)
    parts = jnp.concatenate(
        [high, middle, low, jnp.zeros((5, width), jnp.bfloat16)], axis=0
    )
    moved = lax.dot_general(
        parts, picks, (((1,), (1,)), ((), ())), preferred_element_type=jnp.float32
    )
    return ops, moved[0:1] + moved[1:2] + moved[2:3]


def newton(gram_matrix):
    identity = jnp.eye(gram_matrix.shape[0], dtype=jnp.float32)
    frobenius = jnp.sqrt(jnp.sum(gram_matrix * gram_matrix))
    scaled = gram_matrix / frobenius
    factor = 1.5 * identity - 0.5 * scaled
    scaled = jnp.dot(scaled, factor, precision=lax.Precision.HIGHEST)
    inverse_root = factor
    for repeat in range(1, NS_ITERS):
        factor = 1.5 * identity - 0.5 * jnp.dot(
            inverse_root, scaled, precision=lax.Precision.HIGHEST
        )
        if repeat < NS_ITERS - 1:
            scaled = jnp.dot(scaled, factor, precision=lax.Precision.HIGHEST)
        inverse_root = jnp.dot(factor, inverse_root, precision=lax.Precision.HIGHEST)
    return inverse_root.astype(jnp.bfloat16)


def doubling_sum(value):
    band_size = lax.axis_size("band")
    count = lax.axis_size("dom") * band_size
    bits = list(range(count.bit_length() - 1))
    order = bits[2:3] + bits[0:2] + bits[3:]
    total = value
    for bit in order:
        mask = 1 << bit
        pairs = [(i, i ^ mask) for i in range(count)]
        total = total + lax.ppermute(total, ("dom", "band"), pairs)
    return total


def body(states, cell_kinetic, cell_scale, cell_potential, connectivity, shared_nodes, cell_counts):
    left_face = shared_nodes[0, 0]
    right_face = shared_nodes[0, 1]
    face_width = left_face.shape[0]
    faces = jnp.concatenate([left_face, right_face])
    live_count = cell_counts[0]
    domain = lax.axis_index("dom")
    domains = lax.axis_size("dom")
    node_total = states.shape[1]
    state_cols = states.shape[0]
    has_left = (domain > 0).astype(jnp.float32)
    has_right = (domain < domains - 1).astype(jnp.float32)
    face_counts = jnp.concatenate(
        [jnp.full((face_width,), has_left), jnp.full((face_width,), has_right)]
    )
    node_weight = (
        jnp.ones((node_total,), jnp.float32)
        .at[faces]
        .set(1.0 / (1.0 + face_counts), unique_indices=True)
        .astype(jnp.bfloat16)
    )
    cells, width = connectivity.shape
    starts = jnp.arange(cells, dtype=jnp.int32) * (3 * (width // 4))
    slots = (connectivity - starts[:, None]) % node_total
    alive = (jnp.arange(cells) < live_count).astype(jnp.float32)
    scales = cell_scale * alive
    slot_rows = slots.reshape(cells, 1, width)
    potential_rows = (cell_potential * alive[:, None]).reshape(cells, 1, width)
    up = [(i, i + 1) for i in range(domains - 1)]
    down = [(j, i) for i, j in up]

    def exchange(left_values, right_values):
        from_left = lax.ppermute(right_values, "dom", up)
        from_right = lax.ppermute(left_values, "dom", down)
        return (from_left, from_right)

    first = states.T
    local_sum, *face_values, window_ops, window_pot = field_step(
        faces, scales, slot_rows, potential_rows, vector=first, kinetic=cell_kinetic
    )
    step = functools.partial(field_step, faces, scales, window_ops, window_pot)
    second, local_sum, *face_values = step(local_in=local_sum, received=exchange(*face_values))
    history = [first, second]
    for repeat in range(CHEB - 2):
        following, local_sum, *face_values = step(
            local_in=local_sum, received=exchange(*face_values), older=history[-2], alpha=2.0
        )
        history.append(following)
    (current,) = step(
        local_in=local_sum, received=exchange(*face_values), older=history[-2], alpha=2.0,
        apply=False,
    )
    row_shard = lax.all_to_all(current, "band", split_axis=0, concat_axis=1, tiled=True)
    piece_nodes = row_shard.shape[0]
    weight_rows = lax.dynamic_slice_in_dim(
        node_weight, lax.axis_index("band") * piece_nodes, piece_nodes, 0
    )
    weighted = row_shard * weight_rows[:, None]
    partial_gram = lax.dot_general(
        weighted, row_shard, (((0,), (0,)), ((), ())), preferred_element_type=jnp.float32
    )
    gram_matrix = doubling_sum(partial_gram)
    mixing = newton(gram_matrix)
    rotated = lax.dot_general(
        row_shard, mixing, (((1,), (0,)), ((), ())), preferred_element_type=jnp.float32
    ).astype(jnp.bfloat16)
    back = lax.all_to_all(rotated, "band", split_axis=1, concat_axis=0, tiled=True)
    return back.T


def solution(mesh):
    in_specs = (
        P("band", "dom"),
        P(),
        P("dom"),
        P("dom", None),
        P("dom", None),
        P("dom", None, None),
        P("dom"),
    )
    out_specs = P("band", "dom")
    return jax.shard_map(body, mesh=mesh, in_specs=in_specs, out_specs=out_specs, check_vma=False)
```
